32 devices in a mesh: clips: 2 (over y), frame: 4 (over x, core), row: 4 (over z).
Axes of the slice: x: 2, y: 2, z: 4, core: 2. Of those that a mesh axis runs over, the one named last changes fastest.
Arguments:
- frames: bfloat16 [16, 512, 640], P(('clips', 'frame'), 'row'), parts along dimension 0, may hold values from -16 to 16
- key_index: int32 [4], P('clips'), parts along dimension 0, may hold values from 0 to 7, as said below
- w_query: bfloat16 [640, 640], replicated, may hold values from -0.25 to 0.25
- w_keyval: bfloat16 [640, 1280], replicated, may hold values from -0.25 to 0.25
- w_out: bfloat16 [640, 640], replicated, may hold values from -0.25 to 0.25
- norm_gain: float32 [640], replicated, may hold values from 0.1 to 1.9
- w_first: bfloat16 [3, 640, 640], replicated, may hold values from -0.125 to 0.125
- w_second: bfloat16 [3, 640, 640], replicated, may hold values from -0.125 to 0.125
Outputs:
- edited: bfloat16 [16, 512, 640], P(('clips', 'frame'), 'row'), parts along dimension 0
The draws below stay inside these ranges and needn't reach their ends.
There are 2 independent parts, one for each index of `clips`. The reference program is written for one: setup_inputs(seed, part) draws one part's arguments, and reference() takes and returns one part's arrays. A program takes and returns all parts, laid end to end along the dimension named above; an argument that names none is the same for every part. Nothing has to cross between parts.
Inputs may be any that keep to these rules, and one draw needn't show every extreme that they name: `key_index`: two different frame indices of the window, in either order; one of them is the window's last frame 8 - 1.
All inputs are finite; a program needn't handle non-finite values.
Results may differ from the reference program's by a relative error of at most 0.0067.
Values may be sent and summed in bfloat16 or wider, within the bound.
No kernel may reach another device: no remote copies, remote signals or barrier semaphores. Data moves between devices by JAX's collectives and lax.ppermute only.
A program may use at most 128 MiB of HBM per device.

```python
import jax
import jax.numpy as jnp
from jax import lax

HEADS = 10
HEAD_DIM = 64
C = 640
FRAMES = 8
TOKENS = 512


def draw_frames(key, part):
    shape = (FRAMES, TOKENS, HEADS * HEAD_DIM)
    base = jnp.clip(jax.random.normal(jax.random.fold_in(key, 14), shape, jnp.float32), -6.0, 6.0)
    return base.astype(jnp.bfloat16)


def draw_key_index(key, part):
    mixed_key = jax.random.fold_in(key, part)
    other = jax.random.randint(jax.random.fold_in(mixed_key, 21), (), 0, FRAMES - 1)
    last = jnp.array(FRAMES - 1, jnp.int32)
    coin = jax.random.randint(jax.random.fold_in(key, 22), (), 0, 2)
    flip = (coin + part) % 2
    first = jnp.where(flip == 1, last, other)
    second = jnp.where(flip == 1, other, last)
    return jnp.stack([first, second]).astype(jnp.int32)


def scatter_about(own_key, dims, scale, reach, held_as=jnp.bfloat16):
    return jnp.clip(scale * jax.random.normal(own_key, dims, jnp.float32), -reach, reach).astype(held_as)


def setup_inputs(seed: int = 0, part: int = 0) -> dict:
    arg_keys = jax.random.split(jax.random.key(seed), 9)
    own_keys = jax.random.split(jax.random.fold_in(arg_keys[8], part), 9)
    return {
        "frames": draw_frames(jax.random.fold_in(jax.random.fold_in(arg_keys[8], part), 71), part),
        "key_index": draw_key_index(jax.random.fold_in(jax.random.fold_in(arg_keys[8], part), 71), part),
        "w_query": scatter_about(arg_keys[2], (C, C), C ** -0.5, 0.25),
        "w_keyval": scatter_about(arg_keys[3], (C, 2 * C), C ** -0.5, 0.25),
        "w_out": scatter_about(arg_keys[4], (C, C), C ** -0.5, 0.25),
        "norm_gain": jnp.clip(1.0 + 0.18 * jax.random.normal(arg_keys[5], (C,), jnp.float32), 0.1, 1.9),
        "w_first": scatter_about(arg_keys[6], (3, C, C), (3 * C) ** -0.5, 0.125),
        "w_second": scatter_about(arg_keys[7], (3, C, C), (3 * C) ** -0.5, 0.125),
    }


def temporal_mix(padded, weights, count):
    result = jnp.zeros((count * padded.shape[1], padded.shape[2]), jnp.float32)
    for offset in range(3):
        window = padded[offset:offset + count].reshape(-1, padded.shape[2])
        result = result + jnp.dot(window, weights[offset], preferred_element_type=jnp.float32)
    return result

def reference(frames, key_index, w_query, w_keyval, w_out, norm_gain, w_first, w_second):
    channels = HEADS * HEAD_DIM
    scale = HEAD_DIM ** (-0.5)
    key_frames = frames[key_index.astype(jnp.int32)].reshape(-1, channels)
    keyval = jnp.dot(key_frames, w_keyval, preferred_element_type=jnp.float32).astype(jnp.bfloat16)
    key_heads = keyval[:, :channels].reshape(-1, HEADS, HEAD_DIM).astype(jnp.float32)
    value_heads = keyval[:, channels:].reshape(-1, HEADS, HEAD_DIM).astype(jnp.float32)

    def one_frame(tokens):
        queries = jnp.dot(tokens, w_query, preferred_element_type=jnp.float32).astype(jnp.bfloat16)
        query_heads = queries.reshape(-1, HEADS, HEAD_DIM).astype(jnp.float32)
        scores = jnp.einsum('qhd,khd->hqk', query_heads, key_heads) * scale
        highest = lax.optimization_barrier(jnp.max(scores, axis=-1, keepdims=True))
        exponent = jnp.exp(scores - highest)
        denominator = lax.optimization_barrier(jnp.sum(exponent, axis=-1))
        rounded = lax.optimization_barrier(exponent.astype(jnp.bfloat16))
        weights = rounded.astype(jnp.float32)
        mixed = jnp.einsum('hqk,khd->qhd', weights, value_heads) / denominator.T[:, :, None]
        attended = mixed.reshape(-1, channels).astype(jnp.bfloat16)
        residual = tokens.astype(jnp.float32) + jnp.dot(attended, w_out, preferred_element_type=jnp.float32)
        mean_square = lax.optimization_barrier(jnp.mean(residual * residual, axis=-1, keepdims=True))
        normed = (residual * lax.rsqrt(mean_square + 1e-06) * norm_gain.astype(jnp.float32)).astype(jnp.bfloat16)
        return (residual, normed)
    residual, normed = lax.map(one_frame, frames)
    frame_count = frames.shape[0]
    padded = jnp.pad(normed, ((1, 1), (0, 0), (0, 0)))
    first = temporal_mix(padded, w_first, frame_count)
    hidden = jax.nn.silu(first).astype(jnp.bfloat16).reshape(frame_count, -1, channels)
    padded = jnp.pad(hidden, ((1, 1), (0, 0), (0, 0)))
    second = temporal_mix(padded, w_second, frame_count)
    return (residual.reshape(-1, channels) + second).reshape(frames.shape).astype(jnp.bfloat16)
```

```python
import jax
import jax.numpy as jnp
from jax import lax
from jax.sharding import PartitionSpec as P

HEADS = 10
HEAD_DIM = 64


def extended(array, axis, width):
    size, length = (lax.axis_size(axis), array.shape[0])
    up = [(i, i + 1) for i in range(size - 1)]
    down = [(j, i) for i, j in up]
    last = lax.slice_in_dim(array, length - width, length, axis=0)
    first = lax.slice_in_dim(array, 0, width, axis=0)
    before = lax.ppermute(last, axis, up)
    after = lax.ppermute(first, axis, down)
    return jnp.concatenate([before, array, after], axis=0)


def temporal_mix(padded, weights, count):
    result = jnp.zeros((count * padded.shape[1], padded.shape[2]), jnp.float32)
    for offset in range(3):
        window = padded[offset : offset + count].reshape(-1, padded.shape[2])
        result = result + jnp.dot(window, weights[offset], preferred_element_type=jnp.float32)
    return result


def gather_keyframes(frames, key_index):
    n_loc, rows, channels = frames.shape
    fsize = lax.axis_size("frame")
    rsize = lax.axis_size("row")
    me = lax.axis_index("frame")
    last = n_loc * fsize - 1
    other = key_index[0] + key_index[1] - last
    owner_a = other // n_loc
    cand_a = lax.dynamic_index_in_dim(frames, other % n_loc, 0, keepdims=False)
    cand_b = frames[n_loc - 1]
    owner_b = fsize - 1
    half = rows // 2

    def half_of(x, h):
        return lax.dynamic_slice_in_dim(x, h * half, half, 0)

    got_a = jnp.where(me == owner_a, half_of(cand_a, me % 2), jnp.zeros((half, channels), frames.dtype))
    got_b = half_of(cand_b, me % 2)
    for s in range(1, fsize):
        recv_a = lax.ppermute(
            half_of(cand_a, (me + s) % 2), "frame", [(i, (i + s) % fsize) for i in range(fsize)]
        )
        got_a = jnp.where((me - s) % fsize == owner_a, recv_a, got_a)
        dest = (owner_b + s) % fsize
        recv_b = lax.ppermute(cand_b[(dest % 2) * half : (dest % 2 + 1) * half], "frame", [(owner_b, dest)])
        got_b = jnp.where(me == dest, recv_b, got_b)
    piece = jnp.stack([got_a, got_b])
    pieces = [piece]
    for s in range(1, rsize):
        pieces.append(lax.ppermute(piece, "row", [(i, (i + s) % rsize) for i in range(rsize)]))
    mine = jnp.stack(pieces).reshape(-1, channels)
    sibling = lax.ppermute(mine, "frame", [(i, i ^ 1) for i in range(fsize)])
    return jnp.concatenate([mine, sibling], axis=0)


def shards(frames, key_index, w_query, w_keyval, w_out, norm_gain, w_first, w_second):
    frame_count, row_count, channels = frames.shape
    flattened = frames.reshape(-1, channels)
    queries = jnp.dot(flattened, w_query, preferred_element_type=jnp.float32).astype(jnp.bfloat16)
    query_heads = queries.reshape(-1, HEADS, HEAD_DIM)
    query_total = queries.shape[0]
    key_tokens = gather_keyframes(frames, key_index)
    keyval = jnp.dot(key_tokens, w_keyval, preferred_element_type=jnp.float32).astype(jnp.bfloat16)
    key_heads = keyval[:, :channels].reshape(-1, HEADS, HEAD_DIM)
    value_heads = keyval[:, channels:].reshape(-1, HEADS, HEAD_DIM)
    scores = jnp.einsum(
        "qhd,khd->hqk", query_heads, key_heads, preferred_element_type=jnp.float32
    ) * HEAD_DIM ** (-0.5)
    highest = jnp.max(scores, axis=-1, keepdims=True)
    exponent = jnp.exp(scores - highest)
    denominator = jnp.sum(exponent, axis=-1)
    mixed = jnp.einsum(
        "hqk,khd->qhd", exponent.astype(jnp.bfloat16), value_heads, preferred_element_type=jnp.float32
    )
    mixed = mixed / denominator.T[:, :, None]
    attended = mixed.reshape(query_total, channels).astype(jnp.bfloat16)
    residual = flattened.astype(jnp.float32) + jnp.dot(
        attended, w_out, preferred_element_type=jnp.float32
    )
    mean_square = jnp.mean(residual * residual, axis=-1, keepdims=True)
    normed = (residual * lax.rsqrt(mean_square + 1e-06) * norm_gain).astype(jnp.bfloat16)
    normed = normed.reshape(frame_count, row_count, channels)
    padded = extended(normed, "frame", 1)
    hidden = jax.nn.silu(temporal_mix(padded, w_first, frame_count)).astype(jnp.bfloat16)
    hidden = hidden.reshape(frame_count, row_count, channels)
    padded = extended(hidden, "frame", 1)
    second = temporal_mix(padded, w_second, frame_count)
    return (residual + second).astype(jnp.bfloat16).reshape(frame_count, row_count, channels)


def solution(mesh):
    return jax.shard_map(
        shards,
        mesh=mesh,
        in_specs=(P(("clips", "frame"), "row", None), P("clips"), P(), P(), P(), P(), P(), P()),
        out_specs=P(("clips", "frame"), "row", None),
        check_vma=False,
    )
```

```python
import jax
import jax.numpy as jnp
from jax import lax
from jax.sharding import PartitionSpec as P

HEADS = 10
HEAD_DIM = 64


def extended(array, axis, width):
    size, length = (lax.axis_size(axis), array.shape[0])
    up = [(i, i + 1) for i in range(size - 1)]
    down = [(j, i) for i, j in up]
    last = lax.slice_in_dim(array, length - width, length, axis=0)
    first = lax.slice_in_dim(array, 0, width, axis=0)
    before = lax.ppermute(last, axis, up)
    after = lax.ppermute(first, axis, down)
    return jnp.concatenate([before, array, after], axis=0)


def temporal_mix(padded, weights, count):
    result = jnp.zeros((count * padded.shape[1], padded.shape[2]), jnp.float32)
    for offset in range(3):
        window = padded[offset : offset + count].reshape(-1, padded.shape[2])
        result = result + jnp.dot(window, weights[offset], preferred_element_type=jnp.float32)
    return result


def gather_keyframes(frames, key_index):
    n_loc, rows, channels = frames.shape
    fsize = lax.axis_size("frame")
    rsize = lax.axis_size("row")
    me = lax.axis_index("frame")
    last = n_loc * fsize - 1
    other = key_index[0] + key_index[1] - last
    owner_a = other // n_loc
    cand_a = lax.dynamic_index_in_dim(frames, other % n_loc, 0, keepdims=False)
    cand_b = frames[n_loc - 1]
    owner_b = fsize - 1
    half = rows // 2

    def half_of(x, h):
        return lax.dynamic_slice_in_dim(x, h * half, half, 0)

    own = jnp.stack([half_of(cand_a, me % 2), half_of(cand_b, me % 2)])
    got_a = jnp.where(me == owner_a, own[0], jnp.zeros((half, channels), frames.dtype))
    got_b = own[1]
    for s in range(1, fsize):
        sent = jnp.stack([half_of(cand_a, (me + s) % 2), half_of(cand_b, (me + s) % 2)])
        recv = lax.ppermute(sent, "frame", [(i, (i + s) % fsize) for i in range(fsize)])
        source = (me - s) % fsize
        got_a = jnp.where(source == owner_a, recv[0], got_a)
        got_b = jnp.where(source == owner_b, recv[1], got_b)
    piece = jnp.stack([got_a, got_b])
    pieces = [piece]
    for s in range(1, rsize):
        pieces.append(lax.ppermute(piece, "row", [(i, (i + s) % rsize) for i in range(rsize)]))
    mine = jnp.stack(pieces).reshape(-1, channels)
    sibling = lax.ppermute(mine, "frame", [(i, i ^ 1) for i in range(fsize)])
    return jnp.concatenate([mine, sibling], axis=0)


def shards(frames, key_index, w_query, w_keyval, w_out, norm_gain, w_first, w_second):
    frame_count, row_count, channels = frames.shape
    assert frame_count >= 2
    flattened = frames.reshape(-1, channels)
    queries = jnp.dot(flattened, w_query, preferred_element_type=jnp.float32).astype(jnp.bfloat16)
    query_heads = queries.reshape(-1, HEADS, HEAD_DIM)
    query_total = queries.shape[0]
    key_tokens = gather_keyframes(frames, key_index)
    keyval = jnp.dot(key_tokens, w_keyval, preferred_element_type=jnp.float32).astype(jnp.bfloat16)
    key_heads = keyval[:, :channels].reshape(-1, HEADS, HEAD_DIM)
    value_heads = keyval[:, channels:].reshape(-1, HEADS, HEAD_DIM)
    scores = jnp.einsum(
        "qhd,khd->hqk", query_heads, key_heads, preferred_element_type=jnp.float32
    ) * HEAD_DIM ** (-0.5)
    highest = jnp.max(scores, axis=-1, keepdims=True)
    exponent = jnp.exp(scores - highest)
    denominator = jnp.sum(exponent, axis=-1)
    mixed = jnp.einsum(
        "hqk,khd->qhd", exponent.astype(jnp.bfloat16), value_heads, preferred_element_type=jnp.float32
    )
    mixed = mixed / denominator.T[:, :, None]
    attended = mixed.reshape(query_total, channels).astype(jnp.bfloat16)
    residual = flattened.astype(jnp.float32) + jnp.dot(
        attended, w_out, preferred_element_type=jnp.float32
    )
    mean_square = jnp.mean(residual * residual, axis=-1, keepdims=True)
    normed = (residual * lax.rsqrt(mean_square + 1e-06) * norm_gain).astype(jnp.bfloat16)
    normed = normed.reshape(frame_count, row_count, channels)
    padded = extended(normed, "frame", 2)
    hidden = jax.nn.silu(temporal_mix(padded, w_first, frame_count + 2)).astype(jnp.bfloat16)
    hidden = hidden.reshape(frame_count + 2, row_count, channels)
    me = lax.axis_index("frame")
    outside = jnp.zeros((1, row_count, channels), hidden.dtype)
    hidden = jnp.concatenate(
        [
            jnp.where(me == 0, outside, hidden[:1]),
            hidden[1:-1],
            jnp.where(me == lax.axis_size("frame") - 1, outside, hidden[-1:]),
        ],
        axis=0,
    )
    second = temporal_mix(hidden, w_second, frame_count)
    return (residual + second).astype(jnp.bfloat16).reshape(frame_count, row_count, channels)


def solution(mesh):
    return jax.shard_map(
        shards,
        mesh=mesh,
        in_specs=(P(("clips", "frame"), "row", None), P("clips"), P(), P(), P(), P(), P(), P()),
        out_specs=P(("clips", "frame"), "row", None),
        check_vma=False,
    )
```

```python
import jax
import jax.numpy as jnp
from jax import lax
from jax.experimental import pallas as pl
from jax.sharding import PartitionSpec as P

HEADS = 10
HEAD_DIM = 64


def attention_kernel(q_ref, k_ref, v_ref, o_ref):
    outs = []
    for hh in range(2):
        cols = slice(hh * HEAD_DIM, (hh + 1) * HEAD_DIM)
        scores = lax.dot_general(
            q_ref[:, cols], k_ref[:, cols], (((1,), (1,)), ((), ())),
            preferred_element_type=jnp.float32) * HEAD_DIM ** (-0.5)
        highest = jnp.max(scores, axis=1, keepdims=True)
        exponent = jnp.exp(scores - highest)
        denominator = jnp.sum(exponent, axis=1, keepdims=True)
        mixed = jnp.dot(exponent.astype(jnp.bfloat16), v_ref[:, cols], preferred_element_type=jnp.float32)
        outs.append(mixed / denominator)
    o_ref[...] = jnp.concatenate(outs, axis=1).astype(o_ref.dtype)

def attend(queries, keyval, q_tile=128):
    total, channels = queries.shape
    keys = keyval.shape[0]
    pairs = channels // (2 * HEAD_DIM)
    width = 2 * HEAD_DIM
    return pl.pallas_call(
        attention_kernel,
        grid=(pairs, total // q_tile),
        in_specs=[
            pl.BlockSpec((q_tile, width), lambda j, i: (i, j)),
            pl.BlockSpec((keys, width), lambda j, i: (0, j)),
            pl.BlockSpec((keys, width), lambda j, i: (0, pairs + j)),
        ],
        out_specs=pl.BlockSpec((q_tile, width), lambda j, i: (i, j)),
        out_shape=jax.ShapeDtypeStruct((total, channels), jnp.bfloat16),
    )(queries, keyval, keyval)

def extended(array, axis, width):
    size, length = (lax.axis_size(axis), array.shape[0])
    up = [(i, i + 1) for i in range(size - 1)]
    down = [(j, i) for i, j in up]
    last = lax.slice_in_dim(array, length - width, length, axis=0)
    first = lax.slice_in_dim(array, 0, width, axis=0)
    before = lax.ppermute(last, axis, up)
    after = lax.ppermute(first, axis, down)
    return jnp.concatenate([before, array, after], axis=0)


def temporal_mix(padded, weights, count):
    result = jnp.zeros((count * padded.shape[1], padded.shape[2]), jnp.float32)
    for offset in range(3):
        window = padded[offset : offset + count].reshape(-1, padded.shape[2])
        result = result + jnp.dot(window, weights[offset], preferred_element_type=jnp.float32)
    return result


def gather_keyframes(frames, key_index):
    n_loc, rows, channels = frames.shape
    fsize = lax.axis_size("frame")
    rsize = lax.axis_size("row")
    me = lax.axis_index("frame")
    last = n_loc * fsize - 1
    other = key_index[0] + key_index[1] - last
    owner_a = other // n_loc
    cand_a = lax.dynamic_index_in_dim(frames, other % n_loc, 0, keepdims=False)
    cand_b = frames[n_loc - 1]
    owner_b = fsize - 1
    half = rows // 2

    def half_of(x, h):
        return lax.dynamic_slice_in_dim(x, h * half, half, 0)

    own = jnp.stack([half_of(cand_a, me % 2), half_of(cand_b, me % 2)])
    got_a = jnp.where(me == owner_a, own[0], jnp.zeros((half, channels), frames.dtype))
    got_b = own[1]
    for s in range(1, fsize):
        sent = jnp.stack([half_of(cand_a, (me + s) % 2), half_of(cand_b, (me + s) % 2)])
        recv = lax.ppermute(sent, "frame", [(i, (i + s) % fsize) for i in range(fsize)])
        source = (me - s) % fsize
        got_a = jnp.where(source == owner_a, recv[0], got_a)
        got_b = jnp.where(source == owner_b, recv[1], got_b)
    piece = jnp.stack([got_a, got_b])
    pieces = [piece]
    for s in range(1, rsize):
        pieces.append(lax.ppermute(piece, "row", [(i, (i + s) % rsize) for i in range(rsize)]))
    mine = jnp.stack(pieces).reshape(-1, channels)
    sibling = lax.ppermute(mine, "frame", [(i, i ^ 1) for i in range(fsize)])
    return jnp.concatenate([mine, sibling], axis=0)


def shards(frames, key_index, w_query, w_keyval, w_out, norm_gain, w_first, w_second):
    frame_count, row_count, channels = frames.shape
    assert frame_count >= 2
    flattened = frames.reshape(-1, channels)
    queries = jnp.dot(flattened, w_query, preferred_element_type=jnp.float32).astype(jnp.bfloat16)
    query_total = queries.shape[0]
    key_tokens = gather_keyframes(frames, key_index)
    keyval = jnp.dot(key_tokens, w_keyval, preferred_element_type=jnp.float32).astype(jnp.bfloat16)
    attended = attend(queries, keyval)
    residual = flattened.astype(jnp.float32) + jnp.dot(
        attended, w_out, preferred_element_type=jnp.float32
    )
    mean_square = jnp.mean(residual * residual, axis=-1, keepdims=True)
    normed = (residual * lax.rsqrt(mean_square + 1e-06) * norm_gain).astype(jnp.bfloat16)
    normed = normed.reshape(frame_count, row_count, channels)
    padded = extended(normed, "frame", 2)
    hidden = jax.nn.silu(temporal_mix(padded, w_first, frame_count + 2)).astype(jnp.bfloat16)
    hidden = hidden.reshape(frame_count + 2, row_count, channels)
    me = lax.axis_index("frame")
    outside = jnp.zeros((1, row_count, channels), hidden.dtype)
    hidden = jnp.concatenate(
        [
            jnp.where(me == 0, outside, hidden[:1]),
            hidden[1:-1],
            jnp.where(me == lax.axis_size("frame") - 1, outside, hidden[-1:]),
        ],
        axis=0,
    )
    second = temporal_mix(hidden, w_second, frame_count)
    return (residual + second).astype(jnp.bfloat16).reshape(frame_count, row_count, channels)


def solution(mesh):
    return jax.shard_map(
        shards,
        mesh=mesh,
        in_specs=(P(("clips", "frame"), "row", None), P("clips"), P(), P(), P(), P(), P(), P()),
        out_specs=P(("clips", "frame"), "row", None),
        check_vma=False,
    )
```

```python
import jax
import jax.numpy as jnp
from jax import lax
from jax.experimental import pallas as pl
from jax.sharding import PartitionSpec as P

HEADS = 10
HEAD_DIM = 64


def attention_kernel(q_ref, kt_ref, v_ref, o_ref):
    outs = []
    for hh in range(2):
        cols = slice(hh * HEAD_DIM, (hh + 1) * HEAD_DIM)
        scores = jnp.dot(q_ref[:, cols], kt_ref[cols, :], preferred_element_type=jnp.float32)
        scores = scores * HEAD_DIM ** (-0.5)
        highest = jnp.max(scores, axis=1, keepdims=True)
        exponent = jnp.exp(scores - highest)
        denominator = jnp.sum(exponent, axis=1, keepdims=True)
        mixed = jnp.dot(exponent.astype(jnp.bfloat16), v_ref[:, cols], preferred_element_type=jnp.float32)
        outs.append(mixed / denominator)
    o_ref[...] = jnp.concatenate(outs, axis=1).astype(o_ref.dtype)


def attend(queries, keys_t, values, q_tile=256):
    total, channels = queries.shape
    count = values.shape[0]
    pairs = channels // (2 * HEAD_DIM)
    width = 2 * HEAD_DIM
    return pl.pallas_call(
        attention_kernel,
        grid=(pairs, total // q_tile),
        in_specs=[
            pl.BlockSpec((q_tile, width), lambda j, i: (i, j)),
            pl.BlockSpec((width, count), lambda j, i: (j, 0)),
            pl.BlockSpec((count, width), lambda j, i: (0, j)),
        ],
        out_specs=pl.BlockSpec((q_tile, width), lambda j, i: (i, j)),
        out_shape=jax.ShapeDtypeStruct((total, channels), jnp.bfloat16),
    )(queries, keys_t, values)

def extended(array, axis, width):
    size, length = (lax.axis_size(axis), array.shape[0])
    up = [(i, i + 1) for i in range(size - 1)]
    down = [(j, i) for i, j in up]
    last = lax.slice_in_dim(array, length - width, length, axis=0)
    first = lax.slice_in_dim(array, 0, width, axis=0)
    before = lax.ppermute(last, axis, up)
    after = lax.ppermute(first, axis, down)
    return jnp.concatenate([before, array, after], axis=0)


def temporal_mix(padded, weights, count):
    result = jnp.zeros((count * padded.shape[1], padded.shape[2]), jnp.float32)
    for offset in range(3):
        window = padded[offset : offset + count].reshape(-1, padded.shape[2])
        result = result + jnp.dot(window, weights[offset], preferred_element_type=jnp.float32)
    return result


def gather_keyframes(frames, key_index):
    n_loc, rows, channels = frames.shape
    fsize = lax.axis_size("frame")
    rsize = lax.axis_size("row")
    me = lax.axis_index("frame")
    last = n_loc * fsize - 1
    other = key_index[0] + key_index[1] - last
    owner_a = other // n_loc
    cand_a = lax.dynamic_index_in_dim(frames, other % n_loc, 0, keepdims=False)
    cand_b = frames[n_loc - 1]
    owner_b = fsize - 1
    half = rows // 2

    def half_of(x, h):
        return lax.dynamic_slice_in_dim(x, h * half, half, 0)

    own = jnp.stack([half_of(cand_a, me % 2), half_of(cand_b, me % 2)])
    got_a = jnp.where(me == owner_a, own[0], jnp.zeros((half, channels), frames.dtype))
    got_b = own[1]
    for s in range(1, fsize):
        sent = jnp.stack([half_of(cand_a, (me + s) % 2), half_of(cand_b, (me + s) % 2)])
        recv = lax.ppermute(sent, "frame", [(i, (i + s) % fsize) for i in range(fsize)])
        source = (me - s) % fsize
        got_a = jnp.where(source == owner_a, recv[0], got_a)
        got_b = jnp.where(source == owner_b, recv[1], got_b)
    piece = jnp.stack([got_a, got_b])
    pieces = [piece]
    for s in range(1, rsize):
        pieces.append(lax.ppermute(piece, "row", [(i, (i + s) % rsize) for i in range(rsize)]))
    mine = jnp.stack(pieces).reshape(-1, channels)
    sibling = lax.ppermute(mine, "frame", [(i, i ^ 1) for i in range(fsize)])
    return jnp.concatenate([mine, sibling], axis=0)


def shards(frames, key_index, w_query, w_keyval, w_out, norm_gain, w_first, w_second):
    frame_count, row_count, channels = frames.shape
    assert frame_count >= 2
    flattened = frames.reshape(-1, channels)
    queries = jnp.dot(flattened, w_query, preferred_element_type=jnp.float32).astype(jnp.bfloat16)
    query_total = queries.shape[0]
    key_tokens = gather_keyframes(frames, key_index)
    keys_t = lax.dot_general(
        w_keyval[:, :channels], key_tokens, (((0,), (1,)), ((), ())), preferred_element_type=jnp.float32
    ).astype(jnp.bfloat16)
    values = jnp.dot(key_tokens, w_keyval[:, channels:], preferred_element_type=jnp.float32).astype(jnp.bfloat16)
    attended = attend(queries, keys_t, values)
    residual = flattened.astype(jnp.float32) + jnp.dot(
        attended, w_out, preferred_element_type=jnp.float32
    )
    mean_square = jnp.mean(residual * residual, axis=-1, keepdims=True)
    normed = (residual * lax.rsqrt(mean_square + 1e-06) * norm_gain).astype(jnp.bfloat16)
    normed = normed.reshape(frame_count, row_count, channels)
    padded = extended(normed, "frame", 2)
    hidden = jax.nn.silu(temporal_mix(padded, w_first, frame_count + 2)).astype(jnp.bfloat16)
    hidden = hidden.reshape(frame_count + 2, row_count, channels)
    me = lax.axis_index("frame")
    outside = jnp.zeros((1, row_count, channels), hidden.dtype)
    hidden = jnp.concatenate(
        [
            jnp.where(me == 0, outside, hidden[:1]),
            hidden[1:-1],
            jnp.where(me == lax.axis_size("frame") - 1, outside, hidden[-1:]),
        ],
        axis=0,
    )
    second = temporal_mix(hidden, w_second, frame_count)
    return (residual + second).astype(jnp.bfloat16).reshape(frame_count, row_count, channels)


def solution(mesh):
    return jax.shard_map(
        shards,
        mesh=mesh,
        in_specs=(P(("clips", "frame"), "row", None), P("clips"), P(), P(), P(), P(), P(), P()),
        out_specs=P(("clips", "frame"), "row", None),
        check_vma=False,
    )
```

```python
import jax
import jax.numpy as jnp
from jax import lax
from jax.experimental import pallas as pl
from jax.sharding import PartitionSpec as P

HEADS = 10
HEAD_DIM = 64


def attention_kernel(k_ref, qt_ref, vt_ref, o_ref):
    for hh in range(2):
        cols = slice(hh * HEAD_DIM, (hh + 1) * HEAD_DIM)
        scores = jnp.dot(k_ref[:, cols], qt_ref[cols, :], preferred_element_type=jnp.float32)
        highest = jnp.max(scores, axis=0, keepdims=True)
        exponent = jnp.exp(scores - highest)
        denominator = jnp.sum(exponent, axis=0, keepdims=True)
        mixed = jnp.dot(vt_ref[cols, :], exponent.astype(jnp.bfloat16), preferred_element_type=jnp.float32)
        o_ref[cols, :] = (mixed / denominator).astype(o_ref.dtype)


def attend(keys, queries_t, values_t):
    channels, total = queries_t.shape
    count = keys.shape[0]
    width = 2 * HEAD_DIM
    return pl.pallas_call(
        attention_kernel,
        grid=(channels // width,),
        in_specs=[
            pl.BlockSpec((count, width), lambda j: (0, j)),
            pl.BlockSpec((width, total), lambda j: (j, 0)),
            pl.BlockSpec((width, count), lambda j: (j, 0)),
        ],
        out_specs=pl.BlockSpec((width, total), lambda j: (j, 0)),
        out_shape=jax.ShapeDtypeStruct((channels, total), jnp.bfloat16),
    )(keys, queries_t, values_t)

def extended(array, axis, width):
    size, length = (lax.axis_size(axis), array.shape[0])
    up = [(i, i + 1) for i in range(size - 1)]
    down = [(j, i) for i, j in up]
    last = lax.slice_in_dim(array, length - width, length, axis=0)
    first = lax.slice_in_dim(array, 0, width, axis=0)
    before = lax.ppermute(last, axis, up)
    after = lax.ppermute(first, axis, down)
    return jnp.concatenate([before, array, after], axis=0)


def temporal_mix(padded, weights, count):
    result = jnp.zeros((count * padded.shape[1], padded.shape[2]), jnp.float32)
    for offset in range(3):
        window = padded[offset : offset + count].reshape(-1, padded.shape[2])
        result = result + jnp.dot(window, weights[offset], preferred_element_type=jnp.float32)
    return result


def gather_keyframes(frames, key_index):
    n_loc, rows, channels = frames.shape
    fsize = lax.axis_size("frame")
    rsize = lax.axis_size("row")
    me = lax.axis_index("frame")
    last = n_loc * fsize - 1
    other = key_index[0] + key_index[1] - last
    owner_a = other // n_loc
    cand_a = lax.dynamic_index_in_dim(frames, other % n_loc, 0, keepdims=False)
    cand_b = frames[n_loc - 1]
    owner_b = fsize - 1
    half = rows // 2

    def half_of(x, h):
        return lax.dynamic_slice_in_dim(x, h * half, half, 0)

    own = jnp.stack([half_of(cand_a, me % 2), half_of(cand_b, me % 2)])
    got_a = jnp.where(me == owner_a, own[0], jnp.zeros((half, channels), frames.dtype))
    got_b = own[1]
    for s in range(1, fsize):
        sent = jnp.stack([half_of(cand_a, (me + s) % 2), half_of(cand_b, (me + s) % 2)])
        recv = lax.ppermute(sent, "frame", [(i, (i + s) % fsize) for i in range(fsize)])
        source = (me - s) % fsize
        got_a = jnp.where(source == owner_a, recv[0], got_a)
        got_b = jnp.where(source == owner_b, recv[1], got_b)
    piece = jnp.stack([got_a, got_b])
    pieces = [piece]
    for s in range(1, rsize):
        pieces.append(lax.ppermute(piece, "row", [(i, (i + s) % rsize) for i in range(rsize)]))
    mine = jnp.stack(pieces).reshape(-1, channels)
    sibling = lax.ppermute(mine, "frame", [(i, i ^ 1) for i in range(fsize)])
    return jnp.concatenate([mine, sibling], axis=0)


def shards(frames, key_index, w_query, w_keyval, w_out, norm_gain, w_first, w_second):
    frame_count, row_count, channels = frames.shape
    assert frame_count >= 2
    flattened = frames.reshape(-1, channels)
    queries_t = lax.dot_general(w_query, flattened, (((0,), (1,)), ((), ())), preferred_element_type=jnp.float32)
    queries_t = (queries_t * HEAD_DIM ** (-0.5)).astype(jnp.bfloat16)
    key_tokens = gather_keyframes(frames, key_index)
    keys = jnp.dot(key_tokens, w_keyval[:, :channels], preferred_element_type=jnp.float32).astype(jnp.bfloat16)
    values_t = lax.dot_general(
        w_keyval[:, channels:], key_tokens, (((0,), (1,)), ((), ())), preferred_element_type=jnp.float32
    ).astype(jnp.bfloat16)
    attended_t = attend(keys, queries_t, values_t)
    residual = flattened.astype(jnp.float32) + lax.dot_general(
        attended_t, w_out, (((0,), (0,)), ((), ())), preferred_element_type=jnp.float32
    )
    mean_square = jnp.mean(residual * residual, axis=-1, keepdims=True)
    normed = (residual * lax.rsqrt(mean_square + 1e-06) * norm_gain).astype(jnp.bfloat16)
    normed = normed.reshape(frame_count, row_count, channels)
    padded = extended(normed, "frame", 2)
    hidden = jax.nn.silu(temporal_mix(padded, w_first, frame_count + 2)).astype(jnp.bfloat16)
    hidden = hidden.reshape(frame_count + 2, row_count, channels)
    me = lax.axis_index("frame")
    outside = jnp.zeros((1, row_count, channels), hidden.dtype)
    hidden = jnp.concatenate(
        [
            jnp.where(me == 0, outside, hidden[:1]),
            hidden[1:-1],
            jnp.where(me == lax.axis_size("frame") - 1, outside, hidden[-1:]),
        ],
        axis=0,
    )
    second = temporal_mix(hidden, w_second, frame_count)
    return (residual + second).astype(jnp.bfloat16).reshape(frame_count, row_count, channels)


def solution(mesh):
    return jax.shard_map(
        shards,
        mesh=mesh,
        in_specs=(P(("clips", "frame"), "row", None), P("clips"), P(), P(), P(), P(), P(), P()),
        out_specs=P(("clips", "frame"), "row", None),
        check_vma=False,
    )
```

```python
import jax
import jax.numpy as jnp
from jax import lax
from jax.experimental import pallas as pl
from jax.sharding import PartitionSpec as P

HEADS = 10
HEAD_DIM = 64


def attention_kernel(q_ref, kt_ref, v_ref, o_ref):
    outs = []
    for hh in range(2):
        cols = slice(hh * HEAD_DIM, (hh + 1) * HEAD_DIM)
        scores = jnp.dot(q_ref[:, cols], kt_ref[cols, :], preferred_element_type=jnp.float32)
        scores = scores * HEAD_DIM ** (-0.5)
        highest = jnp.max(scores, axis=1, keepdims=True)
        exponent = jnp.exp(scores - highest)
        denominator = jnp.sum(exponent, axis=1, keepdims=True)
        mixed = jnp.dot(exponent.astype(jnp.bfloat16), v_ref[:, cols], preferred_element_type=jnp.float32)
        outs.append(mixed / denominator)
    o_ref[...] = jnp.concatenate(outs, axis=1).astype(o_ref.dtype)


def attend(queries, keys_t, values, q_tile=256):
    total, channels = queries.shape
    count = values.shape[0]
    pairs = channels // (2 * HEAD_DIM)
    width = 2 * HEAD_DIM
    return pl.pallas_call(
        attention_kernel,
        grid=(pairs, total // q_tile),
        in_specs=[
            pl.BlockSpec((q_tile, width), lambda j, i: (i, j)),
            pl.BlockSpec((width, count), lambda j, i: (j, 0)),
            pl.BlockSpec((count, width), lambda j, i: (0, j)),
        ],
        out_specs=pl.BlockSpec((q_tile, width), lambda j, i: (i, j)),
        out_shape=jax.ShapeDtypeStruct((total, channels), jnp.bfloat16),
    )(queries, keys_t, values)

def extended(array, axis, width):
    size, length = (lax.axis_size(axis), array.shape[0])
    up = [(i, i + 1) for i in range(size - 1)]
    down = [(j, i) for i, j in up]
    last = lax.slice_in_dim(array, length - width, length, axis=0)
    first = lax.slice_in_dim(array, 0, width, axis=0)
    before = lax.ppermute(last, axis, up)
    after = lax.ppermute(first, axis, down)
    return jnp.concatenate([before, array, after], axis=0)


def temporal_mix(padded, weights, count):
    result = jnp.zeros((count * padded.shape[1], padded.shape[2]), jnp.float32)
    for offset in range(3):
        window = padded[offset : offset + count].reshape(-1, padded.shape[2])
        result = result + jnp.dot(window, weights[offset], preferred_element_type=jnp.float32)
    return result


def gather_keyframes(frames, key_index, early):
    n_loc, rows, channels = frames.shape
    fsize = lax.axis_size("frame")
    rsize = lax.axis_size("row")
    me = lax.axis_index("frame")
    last = n_loc * fsize - 1
    other = key_index[0] + key_index[1] - last
    owner_a = other // n_loc
    cand_a = lax.dynamic_index_in_dim(frames, other % n_loc, 0, keepdims=False)
    cand_b = frames[n_loc - 1]
    owner_b = fsize - 1
    half = rows // 2

    def half_of(x, h):
        return lax.dynamic_slice_in_dim(x, h * half, half, 0)

    own = jnp.stack([half_of(cand_a, me % 2), half_of(cand_b, me % 2)])
    got_a = jnp.where(me == owner_a, own[0], jnp.zeros((half, channels), frames.dtype))
    got_b = own[1]
    for s in range(1, fsize):
        sent = jnp.stack([half_of(cand_a, (me + s) % 2), half_of(cand_b, (me + s) % 2)])
        recv = lax.ppermute(sent, "frame", [(i, (i + s) % fsize) for i in range(fsize)])
        source = (me - s) % fsize
        got_a = jnp.where(source == owner_a, recv[0], got_a)
        got_b = jnp.where(source == owner_b, recv[1], got_b)
    piece = jnp.stack([got_a, got_b])
    piece, early = lax.optimization_barrier((piece, early))
    pieces = [piece]
    for s in range(1, rsize):
        pieces.append(lax.ppermute(piece, "row", [(i, (i + s) % rsize) for i in range(rsize)]))
    mine = jnp.stack(pieces).reshape(-1, channels)
    sibling = lax.ppermute(mine, "frame", [(i, i ^ 1) for i in range(fsize)])
    return mine, sibling


def shards(frames, key_index, w_query, w_keyval, w_out, norm_gain, w_first, w_second):
    frame_count, row_count, channels = frames.shape
    assert frame_count >= 2
    flattened = frames.reshape(-1, channels)
    queries = jnp.dot(flattened, w_query, preferred_element_type=jnp.float32).astype(jnp.bfloat16)
    query_total = queries.shape[0]
    mine, sibling = gather_keyframes(frames, key_index, queries)

    def project(tokens):
        keys_t = lax.dot_general(
            w_keyval[:, :channels], tokens, (((0,), (1,)), ((), ())), preferred_element_type=jnp.float32
        ).astype(jnp.bfloat16)
        values = jnp.dot(tokens, w_keyval[:, channels:], preferred_element_type=jnp.float32).astype(jnp.bfloat16)
        return keys_t, values

    keys_mine, values_mine = project(mine)
    keys_sib, values_sib = project(sibling)
    keys_t = jnp.concatenate([keys_mine, keys_sib], axis=1)
    values = jnp.concatenate([values_mine, values_sib], axis=0)
    attended = attend(queries, keys_t, values)
    residual = flattened.astype(jnp.float32) + jnp.dot(
        attended, w_out, preferred_element_type=jnp.float32
    )
    mean_square = jnp.mean(residual * residual, axis=-1, keepdims=True)
    normed = (residual * lax.rsqrt(mean_square + 1e-06) * norm_gain).astype(jnp.bfloat16)
    normed = normed.reshape(frame_count, row_count, channels)
    padded = extended(normed, "frame", 2)
    hidden = jax.nn.silu(temporal_mix(padded, w_first, frame_count + 2)).astype(jnp.bfloat16)
    hidden = hidden.reshape(frame_count + 2, row_count, channels)
    me = lax.axis_index("frame")
    outside = jnp.zeros((1, row_count, channels), hidden.dtype)
    hidden = jnp.concatenate(
        [
            jnp.where(me == 0, outside, hidden[:1]),
            hidden[1:-1],
            jnp.where(me == lax.axis_size("frame") - 1, outside, hidden[-1:]),
        ],
        axis=0,
    )
    second = temporal_mix(hidden, w_second, frame_count)
    return (residual + second).astype(jnp.bfloat16).reshape(frame_count, row_count, channels)


def solution(mesh):
    return jax.shard_map(
        shards,
        mesh=mesh,
        in_specs=(P(("clips", "frame"), "row", None), P("clips"), P(), P(), P(), P(), P(), P()),
        out_specs=P(("clips", "frame"), "row", None),
        check_vma=False,
    )
```

```python
import jax
import jax.numpy as jnp
from jax import lax
from jax.experimental import pallas as pl
from jax.sharding import PartitionSpec as P

HEADS = 10
HEAD_DIM = 64


def attention_kernel(q_ref, kt_ref, v_ref, o_ref):
    outs = []
    for hh in range(2):
        cols = slice(hh * HEAD_DIM, (hh + 1) * HEAD_DIM)
        scores = jnp.dot(q_ref[:, cols], kt_ref[cols, :], preferred_element_type=jnp.float32)
        scores = scores * HEAD_DIM ** (-0.5)
        highest = jnp.max(scores, axis=1, keepdims=True)
        exponent = jnp.exp(scores - highest)
        denominator = jnp.sum(exponent, axis=1, keepdims=True)
        mixed = jnp.dot(exponent.astype(jnp.bfloat16), v_ref[:, cols], preferred_element_type=jnp.float32)
        outs.append(mixed / denominator)
    o_ref[...] = jnp.concatenate(outs, axis=1).astype(o_ref.dtype)


def attend(queries, keys_t, values, q_tile=256):
    total, channels = queries.shape
    count = values.shape[0]
    pairs = channels // (2 * HEAD_DIM)
    width = 2 * HEAD_DIM
    return pl.pallas_call(
        attention_kernel,
        grid=(pairs, total // q_tile),
        in_specs=[
            pl.BlockSpec((q_tile, width), lambda j, i: (i, j)),
            pl.BlockSpec((width, count), lambda j, i: (j, 0)),
            pl.BlockSpec((count, width), lambda j, i: (0, j)),
        ],
        out_specs=pl.BlockSpec((q_tile, width), lambda j, i: (i, j)),
        out_shape=jax.ShapeDtypeStruct((total, channels), jnp.bfloat16),
    )(queries, keys_t, values)

def extended(array, axis, width):
    size, length = (lax.axis_size(axis), array.shape[0])
    up = [(i, i + 1) for i in range(size - 1)]
    down = [(j, i) for i, j in up]
    last = lax.slice_in_dim(array, length - width, length, axis=0)
    first = lax.slice_in_dim(array, 0, width, axis=0)
    before = lax.ppermute(last, axis, up)
    after = lax.ppermute(first, axis, down)
    return jnp.concatenate([before, array, after], axis=0)


def temporal_mix(padded, weights, count):
    result = jnp.zeros((count * padded.shape[1], padded.shape[2]), jnp.float32)
    for offset in range(3):
        window = padded[offset : offset + count].reshape(-1, padded.shape[2])
        result = result + jnp.dot(window, weights[offset], preferred_element_type=jnp.float32)
    return result


def gather_keyframes(frames, key_index, early):
    n_loc, rows, channels = frames.shape
    fsize = lax.axis_size("frame")
    rsize = lax.axis_size("row")
    me = lax.axis_index("frame")
    last = n_loc * fsize - 1
    other = key_index[0] + key_index[1] - last
    owner_a = other // n_loc
    slot_a = other % n_loc
    owner_b = fsize - 1
    half = rows // 2

    def halves(h):
        return lax.dynamic_slice_in_dim(frames, h * half, half, 1)

    own = halves(me % 2)
    got_a = jnp.where(
        me == owner_a, lax.dynamic_index_in_dim(own, slot_a, 0, keepdims=False), jnp.zeros_like(own[0])
    )
    got_b = own[n_loc - 1]
    for s in range(1, fsize):
        recv = lax.ppermute(halves((me + s) % 2), "frame", [(i, (i + s) % fsize) for i in range(fsize)])
        source = (me - s) % fsize
        got_a = jnp.where(source == owner_a, lax.dynamic_index_in_dim(recv, slot_a, 0, keepdims=False), got_a)
        got_b = jnp.where(source == owner_b, recv[n_loc - 1], got_b)
    piece = jnp.stack([got_a, got_b])
    piece, early = lax.optimization_barrier((piece, early))
    pieces = [piece]
    for s in range(1, rsize):
        pieces.append(lax.ppermute(piece, "row", [(i, (i + s) % rsize) for i in range(rsize)]))
    mine = jnp.stack(pieces).reshape(-1, channels)
    sibling = lax.ppermute(mine, "frame", [(i, i ^ 1) for i in range(fsize)])
    return mine, sibling


def shards(frames, key_index, w_query, w_keyval, w_out, norm_gain, w_first, w_second):
    frame_count, row_count, channels = frames.shape
    assert frame_count >= 2
    flattened = frames.reshape(-1, channels)
    queries = jnp.dot(flattened, w_query, preferred_element_type=jnp.float32).astype(jnp.bfloat16)
    query_total = queries.shape[0]
    mine, sibling = gather_keyframes(frames, key_index, queries)

    def project(tokens):
        keys_t = lax.dot_general(
            w_keyval[:, :channels], tokens, (((0,), (1,)), ((), ())), preferred_element_type=jnp.float32
        ).astype(jnp.bfloat16)
        values = jnp.dot(tokens, w_keyval[:, channels:], preferred_element_type=jnp.float32).astype(jnp.bfloat16)
        return keys_t, values

    keys_mine, values_mine = project(mine)
    keys_sib, values_sib = project(sibling)
    keys_t = jnp.concatenate([keys_mine, keys_sib], axis=1)
    values = jnp.concatenate([values_mine, values_sib], axis=0)
    attended = attend(queries, keys_t, values)
    residual = flattened.astype(jnp.float32) + jnp.dot(
        attended, w_out, preferred_element_type=jnp.float32
    )
    mean_square = jnp.mean(residual * residual, axis=-1, keepdims=True)
    normed = (residual * lax.rsqrt(mean_square + 1e-06) * norm_gain).astype(jnp.bfloat16)
    normed = normed.reshape(frame_count, row_count, channels)
    padded = extended(normed, "frame", 2)
    hidden = jax.nn.silu(temporal_mix(padded, w_first, frame_count + 2)).astype(jnp.bfloat16)
    hidden = hidden.reshape(frame_count + 2, row_count, channels)
    me = lax.axis_index("frame")
    outside = jnp.zeros((1, row_count, channels), hidden.dtype)
    hidden = jnp.concatenate(
        [
            jnp.where(me == 0, outside, hidden[:1]),
            hidden[1:-1],
            jnp.where(me == lax.axis_size("frame") - 1, outside, hidden[-1:]),
        ],
        axis=0,
    )
    second = temporal_mix(hidden, w_second, frame_count)
    return (residual + second).astype(jnp.bfloat16).reshape(frame_count, row_count, channels)


def solution(mesh):
    return jax.shard_map(
        shards,
        mesh=mesh,
        in_specs=(P(("clips", "frame"), "row", None), P("clips"), P(), P(), P(), P(), P(), P()),
        out_specs=P(("clips", "frame"), "row", None),
        check_vma=False,
    )
```

```python
import jax
import jax.numpy as jnp
from jax import lax
from jax.experimental import pallas as pl
from jax.sharding import PartitionSpec as P

HEADS = 10
HEAD_DIM = 64


def attention_kernel(q_ref, kt_ref, v_ref, o_ref):
    outs = []
    for hh in range(2):
        cols = slice(hh * HEAD_DIM, (hh + 1) * HEAD_DIM)
        scores = jnp.dot(q_ref[:, cols], kt_ref[cols, :], preferred_element_type=jnp.float32)
        scores = scores * HEAD_DIM ** (-0.5)
        highest = jnp.max(scores, axis=1, keepdims=True)
        exponent = jnp.exp(scores - highest)
        denominator = jnp.sum(exponent, axis=1, keepdims=True)
        mixed = jnp.dot(exponent.astype(jnp.bfloat16), v_ref[:, cols], preferred_element_type=jnp.float32)
        outs.append(mixed / denominator)
    o_ref[...] = jnp.concatenate(outs, axis=1).astype(o_ref.dtype)


def attend(queries, keys_t, values, q_tile=256):
    total, channels = queries.shape
    count = values.shape[0]
    pairs = channels // (2 * HEAD_DIM)
    width = 2 * HEAD_DIM
    return pl.pallas_call(
        attention_kernel,
        grid=(pairs, total // q_tile),
        in_specs=[
            pl.BlockSpec((q_tile, width), lambda j, i: (i, j)),
            pl.BlockSpec((width, count), lambda j, i: (j, 0)),
            pl.BlockSpec((count, width), lambda j, i: (0, j)),
        ],
        out_specs=pl.BlockSpec((q_tile, width), lambda j, i: (i, j)),
        out_shape=jax.ShapeDtypeStruct((total, channels), jnp.bfloat16),
    )(queries, keys_t, values)

def extended(array, axis, width):
    size, length = (lax.axis_size(axis), array.shape[0])
    up = [(i, i + 1) for i in range(size - 1)]
    down = [(j, i) for i, j in up]
    last = lax.slice_in_dim(array, length - width, length, axis=0)
    first = lax.slice_in_dim(array, 0, width, axis=0)
    before = lax.ppermute(last, axis, up)
    after = lax.ppermute(first, axis, down)
    return jnp.concatenate([before, array, after], axis=0)


def temporal_mix(padded, weights, count):
    result = jnp.zeros((count * padded.shape[1], padded.shape[2]), jnp.float32)
    for offset in range(3):
        window = padded[offset : offset + count].reshape(-1, padded.shape[2])
        result = result + jnp.dot(window, weights[offset], preferred_element_type=jnp.float32)
    return result


def gather_keyframes(frames, key_index, early):
    n_loc, rows, channels = frames.shape
    fsize = lax.axis_size("frame")
    rsize = lax.axis_size("row")
    me = lax.axis_index("frame")
    last = n_loc * fsize - 1
    other = key_index[0] + key_index[1] - last
    owner_a = other // n_loc
    slot_a = other % n_loc
    owner_b = fsize - 1
    half = rows // 2
    core = me % 2
    chip = me // 2
    chips = fsize // 2

    def halves(h):
        return lax.dynamic_slice_in_dim(frames, h * half, half, 1)

    from_sibling = lax.ppermute(halves(1 - core), "frame", [(i, i ^ 1) for i in range(fsize)])
    chip_frames = jnp.concatenate([halves(core), from_sibling], axis=0)
    index_a = (owner_a % 2 != core).astype(jnp.int32) * n_loc + slot_a
    index_b = (owner_b % 2 != core).astype(jnp.int32) * n_loc + n_loc - 1
    cand = jnp.stack(
        [
            lax.dynamic_index_in_dim(chip_frames, index_a, 0, keepdims=False),
            lax.dynamic_index_in_dim(chip_frames, index_b, 0, keepdims=False),
        ]
    )
    got_a = cand[0]
    got_b = cand[1]
    for s in range(1, chips):
        recv = lax.ppermute(cand, "frame", [(i, (i + 2 * s) % fsize) for i in range(fsize)])
        source = (chip - s) % chips
        got_a = jnp.where(source == owner_a // 2, recv[0], got_a)
        got_b = jnp.where(source == owner_b // 2, recv[1], got_b)
    piece = jnp.stack([got_a, got_b])
    piece, early = lax.optimization_barrier((piece, early))
    pieces = [piece]
    for s in range(1, rsize):
        pieces.append(lax.ppermute(piece, "row", [(i, (i + s) % rsize) for i in range(rsize)]))
    mine = jnp.stack(pieces).reshape(-1, channels)
    sibling = lax.ppermute(mine, "frame", [(i, i ^ 1) for i in range(fsize)])
    return mine, sibling


def shards(frames, key_index, w_query, w_keyval, w_out, norm_gain, w_first, w_second):
    frame_count, row_count, channels = frames.shape
    assert frame_count >= 2
    flattened = frames.reshape(-1, channels)
    queries = jnp.dot(flattened, w_query, preferred_element_type=jnp.float32).astype(jnp.bfloat16)
    query_total = queries.shape[0]
    mine, sibling = gather_keyframes(frames, key_index, queries)

    def project(tokens):
        keys_t = lax.dot_general(
            w_keyval[:, :channels], tokens, (((0,), (1,)), ((), ())), preferred_element_type=jnp.float32
        ).astype(jnp.bfloat16)
        values = jnp.dot(tokens, w_keyval[:, channels:], preferred_element_type=jnp.float32).astype(jnp.bfloat16)
        return keys_t, values

    keys_mine, values_mine = project(mine)
    keys_sib, values_sib = project(sibling)
    keys_t = jnp.concatenate([keys_mine, keys_sib], axis=1)
    values = jnp.concatenate([values_mine, values_sib], axis=0)
    attended = attend(queries, keys_t, values)
    residual = flattened.astype(jnp.float32) + jnp.dot(
        attended, w_out, preferred_element_type=jnp.float32
    )
    mean_square = jnp.mean(residual * residual, axis=-1, keepdims=True)
    normed = (residual * lax.rsqrt(mean_square + 1e-06) * norm_gain).astype(jnp.bfloat16)
    normed = normed.reshape(frame_count, row_count, channels)
    padded = extended(normed, "frame", 2)
    hidden = jax.nn.silu(temporal_mix(padded, w_first, frame_count + 2)).astype(jnp.bfloat16)
    hidden = hidden.reshape(frame_count + 2, row_count, channels)
    me = lax.axis_index("frame")
    outside = jnp.zeros((1, row_count, channels), hidden.dtype)
    hidden = jnp.concatenate(
        [
            jnp.where(me == 0, outside, hidden[:1]),
            hidden[1:-1],
            jnp.where(me == lax.axis_size("frame") - 1, outside, hidden[-1:]),
        ],
        axis=0,
    )
    second = temporal_mix(hidden, w_second, frame_count)
    return (residual + second).astype(jnp.bfloat16).reshape(frame_count, row_count, channels)


def solution(mesh):
    return jax.shard_map(
        shards,
        mesh=mesh,
        in_specs=(P(("clips", "frame"), "row", None), P("clips"), P(), P(), P(), P(), P(), P()),
        out_specs=P(("clips", "frame"), "row", None),
        check_vma=False,
    )
```

```python
import jax
import jax.numpy as jnp
from jax import lax
from jax.experimental import pallas as pl
from jax.sharding import PartitionSpec as P

HEADS = 10
HEAD_DIM = 64


def attention_kernel(q_ref, kt_ref, v_ref, o_ref):
    outs = []
    for hh in range(2):
        cols = slice(hh * HEAD_DIM, (hh + 1) * HEAD_DIM)
        scores = jnp.dot(q_ref[:, cols], kt_ref[cols, :], preferred_element_type=jnp.float32)
        scores = scores * HEAD_DIM ** (-0.5)
        highest = jnp.max(scores, axis=1, keepdims=True)
        exponent = jnp.exp(scores - highest)
        denominator = jnp.sum(exponent, axis=1, keepdims=True)
        mixed = jnp.dot(exponent.astype(jnp.bfloat16), v_ref[:, cols], preferred_element_type=jnp.float32)
        outs.append(mixed / denominator)
    o_ref[...] = jnp.concatenate(outs, axis=1).astype(o_ref.dtype)


def attend(queries, keys_t, values, q_tile=256):
    total, channels = queries.shape
    count = values.shape[0]
    pairs = channels // (2 * HEAD_DIM)
    width = 2 * HEAD_DIM
    return pl.pallas_call(
        attention_kernel,
        grid=(pairs, total // q_tile),
        in_specs=[
            pl.BlockSpec((q_tile, width), lambda j, i: (i, j)),
            pl.BlockSpec((width, count), lambda j, i: (j, 0)),
            pl.BlockSpec((count, width), lambda j, i: (0, j)),
        ],
        out_specs=pl.BlockSpec((q_tile, width), lambda j, i: (i, j)),
        out_shape=jax.ShapeDtypeStruct((total, channels), jnp.bfloat16),
    )(queries, keys_t, values)

def extended(array, axis, width):
    size, length = (lax.axis_size(axis), array.shape[0])
    up = [(i, i + 1) for i in range(size - 1)]
    down = [(j, i) for i, j in up]
    last = lax.slice_in_dim(array, length - width, length, axis=0)
    first = lax.slice_in_dim(array, 0, width, axis=0)
    before = lax.ppermute(last, axis, up)
    after = lax.ppermute(first, axis, down)
    return jnp.concatenate([before, array, after], axis=0)


def temporal_mix(padded, weights, count):
    result = jnp.zeros((count * padded.shape[1], padded.shape[2]), jnp.float32)
    for offset in range(3):
        window = padded[offset : offset + count].reshape(-1, padded.shape[2])
        result = result + jnp.dot(window, weights[offset], preferred_element_type=jnp.float32)
    return result


def gather_keyframes(frames, key_index, early):
    n_loc, rows, channels = frames.shape
    fsize = lax.axis_size("frame")
    rsize = lax.axis_size("row")
    me = lax.axis_index("frame")
    last = n_loc * fsize - 1
    other = key_index[0] + key_index[1] - last
    owner_a = other // n_loc
    slot_a = other % n_loc
    owner_b = fsize - 1
    half = rows // 2

    def halves(h):
        return lax.dynamic_slice_in_dim(frames, h * half, half, 1)

    own = halves(me % 2)
    got_a = jnp.where(
        me == owner_a, lax.dynamic_index_in_dim(own, slot_a, 0, keepdims=False), jnp.zeros_like(own[0])
    )
    got_b = own[n_loc - 1]
    for s in range(1, fsize):
        recv = lax.ppermute(halves((me + s) % 2), "frame", [(i, (i + s) % fsize) for i in range(fsize)])
        source = (me - s) % fsize
        got_a = jnp.where(source == owner_a, lax.dynamic_index_in_dim(recv, slot_a, 0, keepdims=False), got_a)
        got_b = jnp.where(source == owner_b, recv[n_loc - 1], got_b)
    piece = jnp.stack([got_a, got_b])
    piece, early = lax.optimization_barrier((piece, early))
    copies = jnp.broadcast_to(piece[None], (rsize,) + piece.shape)
    mine = lax.all_to_all(copies, "row", 0, 0, tiled=True).reshape(-1, channels)
    sibling = lax.ppermute(mine, "frame", [(i, i ^ 1) for i in range(fsize)])
    return mine, sibling


def shards(frames, key_index, w_query, w_keyval, w_out, norm_gain, w_first, w_second):
    frame_count, row_count, channels = frames.shape
    assert frame_count >= 2
    flattened = frames.reshape(-1, channels)
    queries = jnp.dot(flattened, w_query, preferred_element_type=jnp.float32).astype(jnp.bfloat16)
    query_total = queries.shape[0]
    mine, sibling = gather_keyframes(frames, key_index, queries)

    def project(tokens):
        keys_t = lax.dot_general(
            w_keyval[:, :channels], tokens, (((0,), (1,)), ((), ())), preferred_element_type=jnp.float32
        ).astype(jnp.bfloat16)
        values = jnp.dot(tokens, w_keyval[:, channels:], preferred_element_type=jnp.float32).astype(jnp.bfloat16)
        return keys_t, values

    keys_mine, values_mine = project(mine)
    keys_sib, values_sib = project(sibling)
    keys_t = jnp.concatenate([keys_mine, keys_sib], axis=1)
    values = jnp.concatenate([values_mine, values_sib], axis=0)
    attended = attend(queries, keys_t, values)
    residual = flattened.astype(jnp.float32) + jnp.dot(
        attended, w_out, preferred_element_type=jnp.float32
    )
    mean_square = jnp.mean(residual * residual, axis=-1, keepdims=True)
    normed = (residual * lax.rsqrt(mean_square + 1e-06) * norm_gain).astype(jnp.bfloat16)
    normed = normed.reshape(frame_count, row_count, channels)
    padded = extended(normed, "frame", 2)
    hidden = jax.nn.silu(temporal_mix(padded, w_first, frame_count + 2)).astype(jnp.bfloat16)
    hidden = hidden.reshape(frame_count + 2, row_count, channels)
    me = lax.axis_index("frame")
    outside = jnp.zeros((1, row_count, channels), hidden.dtype)
    hidden = jnp.concatenate(
        [
            jnp.where(me == 0, outside, hidden[:1]),
            hidden[1:-1],
            jnp.where(me == lax.axis_size("frame") - 1, outside, hidden[-1:]),
        ],
        axis=0,
    )
    second = temporal_mix(hidden, w_second, frame_count)
    return (residual + second).astype(jnp.bfloat16).reshape(frame_count, row_count, channels)


def solution(mesh):
    return jax.shard_map(
        shards,
        mesh=mesh,
        in_specs=(P(("clips", "frame"), "row", None), P("clips"), P(), P(), P(), P(), P(), P()),
        out_specs=P(("clips", "frame"), "row", None),
        check_vma=False,
    )
```

```python
import jax
import jax.numpy as jnp
from jax import lax
from jax.experimental import pallas as pl
from jax.sharding import PartitionSpec as P

HEADS = 10
HEAD_DIM = 64


def attention_kernel(q_ref, kt_a_ref, kt_b_ref, v_a_ref, v_b_ref, o_ref):
    outs = []
    for hh in range(2):
        cols = slice(hh * HEAD_DIM, (hh + 1) * HEAD_DIM)
        query = q_ref[:, cols]
        scores_a = jnp.dot(query, kt_a_ref[cols, :], preferred_element_type=jnp.float32) * HEAD_DIM ** (-0.5)
        scores_b = jnp.dot(query, kt_b_ref[cols, :], preferred_element_type=jnp.float32) * HEAD_DIM ** (-0.5)
        highest = jnp.maximum(
            jnp.max(scores_a, axis=1, keepdims=True), jnp.max(scores_b, axis=1, keepdims=True)
        )
        exponent_a = jnp.exp(scores_a - highest)
        exponent_b = jnp.exp(scores_b - highest)
        denominator = jnp.sum(exponent_a, axis=1, keepdims=True) + jnp.sum(exponent_b, axis=1, keepdims=True)
        mixed = jnp.dot(
            exponent_a.astype(jnp.bfloat16), v_a_ref[:, cols], preferred_element_type=jnp.float32
        ) + jnp.dot(exponent_b.astype(jnp.bfloat16), v_b_ref[:, cols], preferred_element_type=jnp.float32)
        outs.append(mixed / denominator)
    o_ref[...] = jnp.concatenate(outs, axis=1).astype(o_ref.dtype)


def attend(queries, keys_a, keys_b, values_a, values_b):
    total, channels = queries.shape
    count = values_a.shape[0]
    pairs = channels // (2 * HEAD_DIM)
    width = 2 * HEAD_DIM
    key_spec = pl.BlockSpec((width, count), lambda j: (j, 0))
    value_spec = pl.BlockSpec((count, width), lambda j: (0, j))
    return pl.pallas_call(
        attention_kernel,
        grid=(pairs,),
        in_specs=[pl.BlockSpec((total, width), lambda j: (0, j)), key_spec, key_spec, value_spec, value_spec],
        out_specs=pl.BlockSpec((total, width), lambda j: (0, j)),
        out_shape=jax.ShapeDtypeStruct((total, channels), jnp.bfloat16),
    )(queries, keys_a, keys_b, values_a, values_b)


def extended(array, axis, width):
    size, length = (lax.axis_size(axis), array.shape[0])
    up = [(i, i + 1) for i in range(size - 1)]
    down = [(j, i) for i, j in up]
    last = lax.slice_in_dim(array, length - width, length, axis=0)
    first = lax.slice_in_dim(array, 0, width, axis=0)
    before = lax.ppermute(last, axis, up)
    after = lax.ppermute(first, axis, down)
    return jnp.concatenate([before, array, after], axis=0)


def temporal_mix(padded, weights, count):
    result = jnp.zeros((count * padded.shape[1], padded.shape[2]), jnp.float32)
    for offset in range(3):
        window = padded[offset : offset + count].reshape(-1, padded.shape[2])
        result = result + jnp.dot(window, weights[offset], preferred_element_type=jnp.float32)
    return result


def gather_keyframes(frames, key_index, early):
    n_loc, rows, channels = frames.shape
    fsize = lax.axis_size("frame")
    rsize = lax.axis_size("row")
    me = lax.axis_index("frame")
    last = n_loc * fsize - 1
    other = key_index[0] + key_index[1] - last
    owner_a = other // n_loc
    slot_a = other % n_loc
    owner_b = fsize - 1
    half = rows // 2

    def halves(h):
        return lax.dynamic_slice_in_dim(frames, h * half, half, 1)

    own = halves(me % 2)
    got_a = jnp.where(
        me == owner_a, lax.dynamic_index_in_dim(own, slot_a, 0, keepdims=False), jnp.zeros_like(own[0])
    )
    got_b = own[n_loc - 1]
    for s in range(1, fsize):
        recv = lax.ppermute(halves((me + s) % 2), "frame", [(i, (i + s) % fsize) for i in range(fsize)])
        source = (me - s) % fsize
        got_a = jnp.where(source == owner_a, lax.dynamic_index_in_dim(recv, slot_a, 0, keepdims=False), got_a)
        got_b = jnp.where(source == owner_b, recv[n_loc - 1], got_b)
    piece = jnp.stack([got_a, got_b])
    piece, early = lax.optimization_barrier((piece, early))
    pieces = [piece]
    for s in range(1, rsize):
        pieces.append(lax.ppermute(piece, "row", [(i, (i + s) % rsize) for i in range(rsize)]))
    mine = jnp.stack(pieces).reshape(-1, channels)
    sibling = lax.ppermute(mine, "frame", [(i, i ^ 1) for i in range(fsize)])
    return mine, sibling


def shards(frames, key_index, w_query, w_keyval, w_out, norm_gain, w_first, w_second):
    frame_count, row_count, channels = frames.shape
    assert frame_count >= 2
    flattened = frames.reshape(-1, channels)
    queries = jnp.dot(flattened, w_query, preferred_element_type=jnp.float32).astype(jnp.bfloat16)
    query_total = queries.shape[0]
    mine, sibling = gather_keyframes(frames, key_index, queries)

    def project(tokens):
        keys_t = lax.dot_general(
            w_keyval[:, :channels], tokens, (((0,), (1,)), ((), ())), preferred_element_type=jnp.float32
        ).astype(jnp.bfloat16)
        values = jnp.dot(tokens, w_keyval[:, channels:], preferred_element_type=jnp.float32).astype(jnp.bfloat16)
        return keys_t, values

    keys_mine, values_mine = project(mine)
    keys_sib, values_sib = project(sibling)
    attended = attend(queries, keys_mine, keys_sib, values_mine, values_sib)
    residual = flattened.astype(jnp.float32) + jnp.dot(
        attended, w_out, preferred_element_type=jnp.float32
    )
    mean_square = jnp.mean(residual * residual, axis=-1, keepdims=True)
    normed = (residual * lax.rsqrt(mean_square + 1e-06) * norm_gain).astype(jnp.bfloat16)
    normed = normed.reshape(frame_count, row_count, channels)
    padded = extended(normed, "frame", 2)
    hidden = jax.nn.silu(temporal_mix(padded, w_first, frame_count + 2)).astype(jnp.bfloat16)
    hidden = hidden.reshape(frame_count + 2, row_count, channels)
    me = lax.axis_index("frame")
    outside = jnp.zeros((1, row_count, channels), hidden.dtype)
    hidden = jnp.concatenate(
        [
            jnp.where(me == 0, outside, hidden[:1]),
            hidden[1:-1],
            jnp.where(me == lax.axis_size("frame") - 1, outside, hidden[-1:]),
        ],
        axis=0,
    )
    second = temporal_mix(hidden, w_second, frame_count)
    return (residual + second).astype(jnp.bfloat16).reshape(frame_count, row_count, channels)


def solution(mesh):
    return jax.shard_map(
        shards,
        mesh=mesh,
        in_specs=(P(("clips", "frame"), "row", None), P("clips"), P(), P(), P(), P(), P(), P()),
        out_specs=P(("clips", "frame"), "row", None),
        check_vma=False,
    )
```

```python
import jax
import jax.numpy as jnp
from jax import lax
from jax.experimental import pallas as pl
from jax.sharding import PartitionSpec as P

HEADS = 10
HEAD_DIM = 64


def first_chunk_kernel(q_ref, kt_ref, v_ref, m_ref, l_ref, acc_ref):
    for hh in range(2):
        cols = slice(hh * HEAD_DIM, (hh + 1) * HEAD_DIM)
        scores = jnp.dot(q_ref[:, cols], kt_ref[cols, :], preferred_element_type=jnp.float32) * HEAD_DIM ** (-0.5)
        highest = jnp.max(scores, axis=1, keepdims=True)
        exponent = jnp.exp(scores - highest)
        total = jnp.sum(exponent, axis=1, keepdims=True)
        mixed = jnp.dot(exponent.astype(jnp.bfloat16), v_ref[:, cols], preferred_element_type=jnp.float32)
        m_ref[:, cols] = jnp.broadcast_to(highest, mixed.shape)
        l_ref[:, cols] = jnp.broadcast_to(total, mixed.shape)
        acc_ref[:, cols] = mixed


def last_chunk_kernel(q_ref, kt_ref, v_ref, m_ref, l_ref, acc_ref, o_ref):
    outs = []
    for hh in range(2):
        cols = slice(hh * HEAD_DIM, (hh + 1) * HEAD_DIM)
        scores = jnp.dot(q_ref[:, cols], kt_ref[cols, :], preferred_element_type=jnp.float32) * HEAD_DIM ** (-0.5)
        before = jnp.max(m_ref[:, cols], axis=1, keepdims=True)
        highest = jnp.maximum(before, jnp.max(scores, axis=1, keepdims=True))
        kept = jnp.exp(before - highest)
        exponent = jnp.exp(scores - highest)
        total = jnp.max(l_ref[:, cols], axis=1, keepdims=True) * kept + jnp.sum(exponent, axis=1, keepdims=True)
        mixed = acc_ref[:, cols] * kept + jnp.dot(
            exponent.astype(jnp.bfloat16), v_ref[:, cols], preferred_element_type=jnp.float32
        )
        outs.append(mixed / total)
    o_ref[...] = jnp.concatenate(outs, axis=1).astype(o_ref.dtype)


def attend_first(queries, keys_t, values):
    total, channels = queries.shape
    count = values.shape[0]
    width = 2 * HEAD_DIM
    row_spec = pl.BlockSpec((total, width), lambda j: (0, j))
    state = jax.ShapeDtypeStruct((total, channels), jnp.float32)
    return pl.pallas_call(
        first_chunk_kernel,
        grid=(channels // width,),
        in_specs=[row_spec, pl.BlockSpec((width, count), lambda j: (j, 0)), pl.BlockSpec((count, width), lambda j: (0, j))],
        out_specs=[row_spec, row_spec, row_spec],
        out_shape=[state, state, state],
    )(queries, keys_t, values)


def attend_last(queries, keys_t, values, state):
    total, channels = queries.shape
    count = values.shape[0]
    width = 2 * HEAD_DIM
    row_spec = pl.BlockSpec((total, width), lambda j: (0, j))
    return pl.pallas_call(
        last_chunk_kernel,
        grid=(channels // width,),
        in_specs=[row_spec, pl.BlockSpec((width, count), lambda j: (j, 0)), pl.BlockSpec((count, width), lambda j: (0, j))]
        + [row_spec] * 3,
        out_specs=row_spec,
        out_shape=jax.ShapeDtypeStruct((total, channels), jnp.bfloat16),
    )(queries, keys_t, values, *state)

def extended(array, axis, width):
    size, length = (lax.axis_size(axis), array.shape[0])
    up = [(i, i + 1) for i in range(size - 1)]
    down = [(j, i) for i, j in up]
    last = lax.slice_in_dim(array, length - width, length, axis=0)
    first = lax.slice_in_dim(array, 0, width, axis=0)
    before = lax.ppermute(last, axis, up)
    after = lax.ppermute(first, axis, down)
    return jnp.concatenate([before, array, after], axis=0)


def temporal_mix(padded, weights, count):
    result = jnp.zeros((count * padded.shape[1], padded.shape[2]), jnp.float32)
    for offset in range(3):
        window = padded[offset : offset + count].reshape(-1, padded.shape[2])
        result = result + jnp.dot(window, weights[offset], preferred_element_type=jnp.float32)
    return result


def gather_keyframes(frames, key_index, early):
    n_loc, rows, channels = frames.shape
    fsize = lax.axis_size("frame")
    rsize = lax.axis_size("row")
    me = lax.axis_index("frame")
    last = n_loc * fsize - 1
    other = key_index[0] + key_index[1] - last
    owner_a = other // n_loc
    slot_a = other % n_loc
    owner_b = fsize - 1
    half = rows // 2

    def halves(h):
        return lax.dynamic_slice_in_dim(frames, h * half, half, 1)

    own = halves(me % 2)
    got_a = jnp.where(
        me == owner_a, lax.dynamic_index_in_dim(own, slot_a, 0, keepdims=False), jnp.zeros_like(own[0])
    )
    got_b = own[n_loc - 1]
    for s in range(1, fsize):
        recv = lax.ppermute(halves((me + s) % 2), "frame", [(i, (i + s) % fsize) for i in range(fsize)])
        source = (me - s) % fsize
        got_a = jnp.where(source == owner_a, lax.dynamic_index_in_dim(recv, slot_a, 0, keepdims=False), got_a)
        got_b = jnp.where(source == owner_b, recv[n_loc - 1], got_b)
    piece = jnp.stack([got_a, got_b])
    piece, early = lax.optimization_barrier((piece, early))
    swap = [(i, i ^ 1) for i in range(fsize)]
    own_row = jnp.concatenate([piece, lax.ppermute(piece, "frame", swap)], axis=0).reshape(-1, channels)
    pieces = []
    for s in range(1, rsize):
        pieces.append(lax.ppermute(piece, "row", [(i, (i + s) % rsize) for i in range(rsize)]))
    return own_row, pieces


def shards(frames, key_index, w_query, w_keyval, w_out, norm_gain, w_first, w_second):
    frame_count, row_count, channels = frames.shape
    assert frame_count >= 2
    flattened = frames.reshape(-1, channels)
    queries = jnp.dot(flattened, w_query, preferred_element_type=jnp.float32).astype(jnp.bfloat16)
    query_total = queries.shape[0]
    own_row, pieces = gather_keyframes(frames, key_index, queries)

    def project(tokens):
        keys_t = lax.dot_general(
            w_keyval[:, :channels], tokens, (((0,), (1,)), ((), ())), preferred_element_type=jnp.float32
        ).astype(jnp.bfloat16)
        values = jnp.dot(tokens, w_keyval[:, channels:], preferred_element_type=jnp.float32).astype(jnp.bfloat16)
        return keys_t, values

    state = attend_first(queries, *project(own_row))
    pieces, state = lax.optimization_barrier((pieces, state))
    mine = jnp.stack(pieces).reshape(-1, channels)
    sibling = lax.ppermute(mine, "frame", [(i, i ^ 1) for i in range(lax.axis_size("frame"))])
    keys_mine, values_mine = project(mine)
    keys_sib, values_sib = project(sibling)
    keys_t = jnp.concatenate([keys_mine, keys_sib], axis=1)
    values = jnp.concatenate([values_mine, values_sib], axis=0)
    attended = attend_last(queries, keys_t, values, state)
    residual = flattened.astype(jnp.float32) + jnp.dot(
        attended, w_out, preferred_element_type=jnp.float32
    )
    mean_square = jnp.mean(residual * residual, axis=-1, keepdims=True)
    normed = (residual * lax.rsqrt(mean_square + 1e-06) * norm_gain).astype(jnp.bfloat16)
    normed = normed.reshape(frame_count, row_count, channels)
    padded = extended(normed, "frame", 2)
    hidden = jax.nn.silu(temporal_mix(padded, w_first, frame_count + 2)).astype(jnp.bfloat16)
    hidden = hidden.reshape(frame_count + 2, row_count, channels)
    me = lax.axis_index("frame")
    outside = jnp.zeros((1, row_count, channels), hidden.dtype)
    hidden = jnp.concatenate(
        [
            jnp.where(me == 0, outside, hidden[:1]),
            hidden[1:-1],
            jnp.where(me == lax.axis_size("frame") - 1, outside, hidden[-1:]),
        ],
        axis=0,
    )
    second = temporal_mix(hidden, w_second, frame_count)
    return (residual + second).astype(jnp.bfloat16).reshape(frame_count, row_count, channels)


def solution(mesh):
    return jax.shard_map(
        shards,
        mesh=mesh,
        in_specs=(P(("clips", "frame"), "row", None), P("clips"), P(), P(), P(), P(), P(), P()),
        out_specs=P(("clips", "frame"), "row", None),
        check_vma=False,
    )
```

```python
import jax
import jax.numpy as jnp
from jax import lax
from jax.experimental import pallas as pl
from jax.sharding import PartitionSpec as P

HEADS = 10
HEAD_DIM = 64


def attention_kernel(q_ref, kt_ref, v_ref, o_ref):
    heads = [slice(h * HEAD_DIM, (h + 1) * HEAD_DIM) for h in range(q_ref.shape[1] // HEAD_DIM)]
    scores = [
        jnp.dot(q_ref[:, c], kt_ref[c, :], preferred_element_type=jnp.float32) * HEAD_DIM ** (-0.5) for c in heads
    ]
    highest = [jnp.max(s, axis=1, keepdims=True) for s in scores]
    exponent = [jnp.exp(s - m) for s, m in zip(scores, highest)]
    denominator = [jnp.sum(e, axis=1, keepdims=True) for e in exponent]
    mixed = [
        jnp.dot(e.astype(jnp.bfloat16), v_ref[:, c], preferred_element_type=jnp.float32)
        for e, c in zip(exponent, heads)
    ]
    o_ref[...] = jnp.concatenate([m / d for m, d in zip(mixed, denominator)], axis=1).astype(o_ref.dtype)


def attend(queries, keys_t, values):
    total, channels = queries.shape
    count = values.shape[0]
    width = channels if total * count * channels <= 256 * 1024 * 640 else 2 * HEAD_DIM
    return pl.pallas_call(
        attention_kernel,
        grid=(channels // width,),
        in_specs=[
            pl.BlockSpec((total, width), lambda j: (0, j)),
            pl.BlockSpec((width, count), lambda j: (j, 0)),
            pl.BlockSpec((count, width), lambda j: (0, j)),
        ],
        out_specs=pl.BlockSpec((total, width), lambda j: (0, j)),
        out_shape=jax.ShapeDtypeStruct((total, channels), jnp.bfloat16),
    )(queries, keys_t, values)


def extended(array, axis, width):
    size, length = (lax.axis_size(axis), array.shape[0])
    up = [(i, i + 1) for i in range(size - 1)]
    down = [(j, i) for i, j in up]
    last = lax.slice_in_dim(array, length - width, length, axis=0)
    first = lax.slice_in_dim(array, 0, width, axis=0)
    before = lax.ppermute(last, axis, up)
    after = lax.ppermute(first, axis, down)
    return jnp.concatenate([before, array, after], axis=0)


def temporal_mix(padded, weights, count):
    result = jnp.zeros((count * padded.shape[1], padded.shape[2]), jnp.float32)
    for offset in range(3):
        window = padded[offset : offset + count].reshape(-1, padded.shape[2])
        result = result + jnp.dot(window, weights[offset], preferred_element_type=jnp.float32)
    return result


def gather_keyframes(frames, key_index, early):
    n_loc, rows, channels = frames.shape
    fsize = lax.axis_size("frame")
    rsize = lax.axis_size("row")
    me = lax.axis_index("frame")
    last = n_loc * fsize - 1
    other = key_index[0] + key_index[1] - last
    owner_a = other // n_loc
    slot_a = other % n_loc
    owner_b = fsize - 1
    half = rows // 2

    def halves(h):
        return lax.dynamic_slice_in_dim(frames, h * half, half, 1)

    own = halves(me % 2)
    got_a = jnp.where(
        me == owner_a, lax.dynamic_index_in_dim(own, slot_a, 0, keepdims=False), jnp.zeros_like(own[0])
    )
    got_b = own[n_loc - 1]
    for s in range(1, fsize):
        recv = lax.ppermute(halves((me + s) % 2), "frame", [(i, (i + s) % fsize) for i in range(fsize)])
        source = (me - s) % fsize
        got_a = jnp.where(source == owner_a, lax.dynamic_index_in_dim(recv, slot_a, 0, keepdims=False), got_a)
        got_b = jnp.where(source == owner_b, recv[n_loc - 1], got_b)
    piece = jnp.stack([got_a, got_b])
    piece, early = lax.optimization_barrier((piece, early))
    pieces = [piece]
    for s in range(1, rsize):
        pieces.append(lax.ppermute(piece, "row", [(i, (i + s) % rsize) for i in range(rsize)]))
    mine = jnp.stack(pieces).reshape(-1, channels)
    sibling = lax.ppermute(mine, "frame", [(i, i ^ 1) for i in range(fsize)])
    return mine, sibling


def shards(frames, key_index, w_query, w_keyval, w_out, norm_gain, w_first, w_second):
    frame_count, row_count, channels = frames.shape
    assert frame_count >= 2
    flattened = frames.reshape(-1, channels)
    queries = jnp.dot(flattened, w_query, preferred_element_type=jnp.float32).astype(jnp.bfloat16)
    query_total = queries.shape[0]
    mine, sibling = gather_keyframes(frames, key_index, queries)

    def project(tokens):
        keys_t = lax.dot_general(
            w_keyval[:, :channels], tokens, (((0,), (1,)), ((), ())), preferred_element_type=jnp.float32
        ).astype(jnp.bfloat16)
        values = jnp.dot(tokens, w_keyval[:, channels:], preferred_element_type=jnp.float32).astype(jnp.bfloat16)
        return keys_t, values

    keys_mine, values_mine = project(mine)
    keys_sib, values_sib = project(sibling)
    keys_t = jnp.concatenate([keys_mine, keys_sib], axis=1)
    values = jnp.concatenate([values_mine, values_sib], axis=0)
    attended = attend(queries, keys_t, values)
    residual = flattened.astype(jnp.float32) + jnp.dot(
        attended, w_out, preferred_element_type=jnp.float32
    )
    mean_square = jnp.mean(residual * residual, axis=-1, keepdims=True)
    normed = (residual * lax.rsqrt(mean_square + 1e-06) * norm_gain).astype(jnp.bfloat16)
    normed = normed.reshape(frame_count, row_count, channels)
    padded = extended(normed, "frame", 2)
    hidden = jax.nn.silu(temporal_mix(padded, w_first, frame_count + 2)).astype(jnp.bfloat16)
    hidden = hidden.reshape(frame_count + 2, row_count, channels)
    me = lax.axis_index("frame")
    outside = jnp.zeros((1, row_count, channels), hidden.dtype)
    hidden = jnp.concatenate(
        [
            jnp.where(me == 0, outside, hidden[:1]),
            hidden[1:-1],
            jnp.where(me == lax.axis_size("frame") - 1, outside, hidden[-1:]),
        ],
        axis=0,
    )
    second = temporal_mix(hidden, w_second, frame_count)
    return (residual + second).astype(jnp.bfloat16).reshape(frame_count, row_count, channels)


def solution(mesh):
    return jax.shard_map(
        shards,
        mesh=mesh,
        in_specs=(P(("clips", "frame"), "row", None), P("clips"), P(), P(), P(), P(), P(), P()),
        out_specs=P(("clips", "frame"), "row", None),
        check_vma=False,
    )
```

```python
import jax
import jax.numpy as jnp
from jax import lax
from jax.experimental import pallas as pl
from jax.sharding import PartitionSpec as P

HEADS = 10
HEAD_DIM = 64


def attention_kernel(q_ref, kt_ref, v_ref, o_ref):
    heads = [slice(h * HEAD_DIM, (h + 1) * HEAD_DIM) for h in range(q_ref.shape[1] // HEAD_DIM)]
    scores = [
        jnp.dot(q_ref[:, c], kt_ref[c, :], preferred_element_type=jnp.float32) * HEAD_DIM ** (-0.5) for c in heads
    ]
    highest = [jnp.max(s, axis=1, keepdims=True) for s in scores]
    exponent = [jnp.exp(s - m) for s, m in zip(scores, highest)]
    denominator = [jnp.sum(e, axis=1, keepdims=True) for e in exponent]
    mixed = [
        jnp.dot(e.astype(jnp.bfloat16), v_ref[:, c], preferred_element_type=jnp.float32)
        for e, c in zip(exponent, heads)
    ]
    o_ref[...] = jnp.concatenate([m / d for m, d in zip(mixed, denominator)], axis=1).astype(o_ref.dtype)


def attend(queries, keys_t, values):
    total, channels = queries.shape
    count = values.shape[0]
    width = channels if total * count * channels <= 256 * 1024 * 640 else 2 * HEAD_DIM
    return pl.pallas_call(
        attention_kernel,
        grid=(channels // width,),
        in_specs=[
            pl.BlockSpec((total, width), lambda j: (0, j)),
            pl.BlockSpec((width, count), lambda j: (j, 0)),
            pl.BlockSpec((count, width), lambda j: (0, j)),
        ],
        out_specs=pl.BlockSpec((total, width), lambda j: (0, j)),
        out_shape=jax.ShapeDtypeStruct((total, channels), jnp.bfloat16),
    )(queries, keys_t, values)


def extended(array, axis, width):
    size, length = (lax.axis_size(axis), array.shape[0])
    up = [(i, i + 1) for i in range(size - 1)]
    down = [(j, i) for i, j in up]
    last = lax.slice_in_dim(array, length - width, length, axis=0)
    first = lax.slice_in_dim(array, 0, width, axis=0)
    before = lax.ppermute(last, axis, up)
    after = lax.ppermute(first, axis, down)
    return jnp.concatenate([before, array, after], axis=0)


def temporal_mix(padded, weights, count):
    windows = jnp.concatenate([padded[offset : offset + count] for offset in range(3)], axis=-1)
    stacked = weights.reshape(-1, weights.shape[-1])
    return jnp.dot(windows.reshape(-1, stacked.shape[0]), stacked, preferred_element_type=jnp.float32)


def gather_keyframes(frames, key_index, early):
    n_loc, rows, channels = frames.shape
    fsize = lax.axis_size("frame")
    rsize = lax.axis_size("row")
    me = lax.axis_index("frame")
    last = n_loc * fsize - 1
    other = key_index[0] + key_index[1] - last
    owner_a = other // n_loc
    slot_a = other % n_loc
    owner_b = fsize - 1
    half = rows // 2

    def halves(h):
        return lax.dynamic_slice_in_dim(frames, h * half, half, 1)

    own = halves(me % 2)
    got_a = jnp.where(
        me == owner_a, lax.dynamic_index_in_dim(own, slot_a, 0, keepdims=False), jnp.zeros_like(own[0])
    )
    got_b = own[n_loc - 1]
    for s in range(1, fsize):
        recv = lax.ppermute(halves((me + s) % 2), "frame", [(i, (i + s) % fsize) for i in range(fsize)])
        source = (me - s) % fsize
        got_a = jnp.where(source == owner_a, lax.dynamic_index_in_dim(recv, slot_a, 0, keepdims=False), got_a)
        got_b = jnp.where(source == owner_b, recv[n_loc - 1], got_b)
    piece = jnp.stack([got_a, got_b])
    piece, early = lax.optimization_barrier((piece, early))
    pieces = [piece]
    for s in range(1, rsize):
        pieces.append(lax.ppermute(piece, "row", [(i, (i + s) % rsize) for i in range(rsize)]))
    mine = jnp.stack(pieces).reshape(-1, channels)
    sibling = lax.ppermute(mine, "frame", [(i, i ^ 1) for i in range(fsize)])
    return mine, sibling


def shards(frames, key_index, w_query, w_keyval, w_out, norm_gain, w_first, w_second):
    frame_count, row_count, channels = frames.shape
    assert frame_count >= 2
    flattened = frames.reshape(-1, channels)
    queries = jnp.dot(flattened, w_query, preferred_element_type=jnp.float32).astype(jnp.bfloat16)
    query_total = queries.shape[0]
    mine, sibling = gather_keyframes(frames, key_index, queries)

    def project(tokens):
        keys_t = lax.dot_general(
            w_keyval[:, :channels], tokens, (((0,), (1,)), ((), ())), preferred_element_type=jnp.float32
        ).astype(jnp.bfloat16)
        values = jnp.dot(tokens, w_keyval[:, channels:], preferred_element_type=jnp.float32).astype(jnp.bfloat16)
        return keys_t, values

    keys_mine, values_mine = project(mine)
    keys_sib, values_sib = project(sibling)
    keys_t = jnp.concatenate([keys_mine, keys_sib], axis=1)
    values = jnp.concatenate([values_mine, values_sib], axis=0)
    attended = attend(queries, keys_t, values)
    residual = flattened.astype(jnp.float32) + jnp.dot(
        attended, w_out, preferred_element_type=jnp.float32
    )
    mean_square = jnp.mean(residual * residual, axis=-1, keepdims=True)
    normed = (residual * lax.rsqrt(mean_square + 1e-06) * norm_gain).astype(jnp.bfloat16)
    normed = normed.reshape(frame_count, row_count, channels)
    padded = extended(normed, "frame", 2)
    hidden = jax.nn.silu(temporal_mix(padded, w_first, frame_count + 2)).astype(jnp.bfloat16)
    hidden = hidden.reshape(frame_count + 2, row_count, channels)
    me = lax.axis_index("frame")
    outside = jnp.zeros((1, row_count, channels), hidden.dtype)
    hidden = jnp.concatenate(
        [
            jnp.where(me == 0, outside, hidden[:1]),
            hidden[1:-1],
            jnp.where(me == lax.axis_size("frame") - 1, outside, hidden[-1:]),
        ],
        axis=0,
    )
    second = temporal_mix(hidden, w_second, frame_count)
    return (residual + second).astype(jnp.bfloat16).reshape(frame_count, row_count, channels)


def solution(mesh):
    return jax.shard_map(
        shards,
        mesh=mesh,
        in_specs=(P(("clips", "frame"), "row", None), P("clips"), P(), P(), P(), P(), P(), P()),
        out_specs=P(("clips", "frame"), "row", None),
        check_vma=False,
    )
```

```python
import jax
import jax.numpy as jnp
from jax import lax
from jax.experimental import pallas as pl
from jax.sharding import PartitionSpec as P

HEADS = 10
HEAD_DIM = 64


def attention_kernel(k_ref, qt_ref, vt_ref, o_ref):
    heads = [slice(h * HEAD_DIM, (h + 1) * HEAD_DIM) for h in range(qt_ref.shape[0] // HEAD_DIM)]
    scores = [jnp.dot(k_ref[:, c], qt_ref[c, :], preferred_element_type=jnp.float32) for c in heads]
    highest = [jnp.max(s, axis=0, keepdims=True) for s in scores]
    exponent = [jnp.exp(s - m) for s, m in zip(scores, highest)]
    denominator = [jnp.sum(e, axis=0, keepdims=True) for e in exponent]
    mixed = [
        jnp.dot(vt_ref[c, :], e.astype(jnp.bfloat16), preferred_element_type=jnp.float32)
        for e, c in zip(exponent, heads)
    ]
    o_ref[...] = jnp.concatenate([m / d for m, d in zip(mixed, denominator)], axis=0).astype(o_ref.dtype)


def attend(keys, queries_t, values_t):
    channels, total = queries_t.shape
    count = keys.shape[0]
    width = channels if total * count * channels <= 256 * 1024 * 640 else 2 * HEAD_DIM
    return pl.pallas_call(
        attention_kernel,
        grid=(channels // width,),
        in_specs=[
            pl.BlockSpec((count, width), lambda j: (0, j)),
            pl.BlockSpec((width, total), lambda j: (j, 0)),
            pl.BlockSpec((width, count), lambda j: (j, 0)),
        ],
        out_specs=pl.BlockSpec((width, total), lambda j: (j, 0)),
        out_shape=jax.ShapeDtypeStruct((channels, total), jnp.bfloat16),
    )(keys, queries_t, values_t)


def extended(array, axis, width):
    size, length = (lax.axis_size(axis), array.shape[0])
    up = [(i, i + 1) for i in range(size - 1)]
    down = [(j, i) for i, j in up]
    last = lax.slice_in_dim(array, length - width, length, axis=0)
    first = lax.slice_in_dim(array, 0, width, axis=0)
    before = lax.ppermute(last, axis, up)
    after = lax.ppermute(first, axis, down)
    return jnp.concatenate([before, array, after], axis=0)


def temporal_mix(padded, weights, count):
    result = jnp.zeros((count * padded.shape[1], padded.shape[2]), jnp.float32)
    for offset in range(3):
        window = padded[offset : offset + count].reshape(-1, padded.shape[2])
        result = result + jnp.dot(window, weights[offset], preferred_element_type=jnp.float32)
    return result


def gather_keyframes(frames, key_index, early):
    n_loc, rows, channels = frames.shape
    fsize = lax.axis_size("frame")
    rsize = lax.axis_size("row")
    me = lax.axis_index("frame")
    last = n_loc * fsize - 1
    other = key_index[0] + key_index[1] - last
    owner_a = other // n_loc
    slot_a = other % n_loc
    owner_b = fsize - 1
    half = rows // 2

    def halves(h):
        return lax.dynamic_slice_in_dim(frames, h * half, half, 1)

    own = halves(me % 2)
    got_a = jnp.where(
        me == owner_a, lax.dynamic_index_in_dim(own, slot_a, 0, keepdims=False), jnp.zeros_like(own[0])
    )
    got_b = own[n_loc - 1]
    for s in range(1, fsize):
        recv = lax.ppermute(halves((me + s) % 2), "frame", [(i, (i + s) % fsize) for i in range(fsize)])
        source = (me - s) % fsize
        got_a = jnp.where(source == owner_a, lax.dynamic_index_in_dim(recv, slot_a, 0, keepdims=False), got_a)
        got_b = jnp.where(source == owner_b, recv[n_loc - 1], got_b)
    piece = jnp.stack([got_a, got_b])
    piece, early = lax.optimization_barrier((piece, early))
    pieces = [piece]
    for s in range(1, rsize):
        pieces.append(lax.ppermute(piece, "row", [(i, (i + s) % rsize) for i in range(rsize)]))
    mine = jnp.stack(pieces).reshape(-1, channels)
    sibling = lax.ppermute(mine, "frame", [(i, i ^ 1) for i in range(fsize)])
    return mine, sibling


def shards(frames, key_index, w_query, w_keyval, w_out, norm_gain, w_first, w_second):
    frame_count, row_count, channels = frames.shape
    assert frame_count >= 2
    flattened = frames.reshape(-1, channels)
    queries_t = lax.dot_general(w_query, flattened, (((0,), (1,)), ((), ())), preferred_element_type=jnp.float32)
    queries_t = (queries_t * HEAD_DIM ** (-0.5)).astype(jnp.bfloat16)
    mine, sibling = gather_keyframes(frames, key_index, queries_t)

    def project(tokens):
        keys = jnp.dot(tokens, w_keyval[:, :channels], preferred_element_type=jnp.float32).astype(jnp.bfloat16)
        values_t = lax.dot_general(
            w_keyval[:, channels:], tokens, (((0,), (1,)), ((), ())), preferred_element_type=jnp.float32
        ).astype(jnp.bfloat16)
        return keys, values_t

    keys_mine, values_mine = project(mine)
    keys_sib, values_sib = project(sibling)
    keys = jnp.concatenate([keys_mine, keys_sib], axis=0)
    values_t = jnp.concatenate([values_mine, values_sib], axis=1)
    attended_t = attend(keys, queries_t, values_t)
    residual = flattened.astype(jnp.float32) + lax.dot_general(
        attended_t, w_out, (((0,), (0,)), ((), ())), preferred_element_type=jnp.float32
    )
    mean_square = jnp.mean(residual * residual, axis=-1, keepdims=True)
    normed = (residual * lax.rsqrt(mean_square + 1e-06) * norm_gain).astype(jnp.bfloat16)
    normed = normed.reshape(frame_count, row_count, channels)
    padded = extended(normed, "frame", 2)
    hidden = jax.nn.silu(temporal_mix(padded, w_first, frame_count + 2)).astype(jnp.bfloat16)
    hidden = hidden.reshape(frame_count + 2, row_count, channels)
    me = lax.axis_index("frame")
    outside = jnp.zeros((1, row_count, channels), hidden.dtype)
    hidden = jnp.concatenate(
        [
            jnp.where(me == 0, outside, hidden[:1]),
            hidden[1:-1],
            jnp.where(me == lax.axis_size("frame") - 1, outside, hidden[-1:]),
        ],
        axis=0,
    )
    second = temporal_mix(hidden, w_second, frame_count)
    return (residual + second).astype(jnp.bfloat16).reshape(frame_count, row_count, channels)


def solution(mesh):
    return jax.shard_map(
        shards,
        mesh=mesh,
        in_specs=(P(("clips", "frame"), "row", None), P("clips"), P(), P(), P(), P(), P(), P()),
        out_specs=P(("clips", "frame"), "row", None),
        check_vma=False,
    )
```

```python
import jax
import jax.numpy as jnp
from jax import lax
from jax.experimental import pallas as pl
from jax.sharding import PartitionSpec as P

HEADS = 10
HEAD_DIM = 64


def attention_kernel(k_a_ref, k_b_ref, qt_ref, vt_a_ref, vt_b_ref, o_ref):
    heads = [slice(h * HEAD_DIM, (h + 1) * HEAD_DIM) for h in range(qt_ref.shape[0] // HEAD_DIM)]
    scores_a = [jnp.dot(k_a_ref[:, c], qt_ref[c, :], preferred_element_type=jnp.float32) for c in heads]
    scores_b = [jnp.dot(k_b_ref[:, c], qt_ref[c, :], preferred_element_type=jnp.float32) for c in heads]
    highest = [
        jnp.maximum(jnp.max(a, axis=0, keepdims=True), jnp.max(b, axis=0, keepdims=True))
        for a, b in zip(scores_a, scores_b)
    ]
    exp_a = [jnp.exp(a - m) for a, m in zip(scores_a, highest)]
    exp_b = [jnp.exp(b - m) for b, m in zip(scores_b, highest)]
    denominator = [
        jnp.sum(a, axis=0, keepdims=True) + jnp.sum(b, axis=0, keepdims=True) for a, b in zip(exp_a, exp_b)
    ]
    mixed = [
        jnp.dot(vt_a_ref[c, :], a.astype(jnp.bfloat16), preferred_element_type=jnp.float32)
        + jnp.dot(vt_b_ref[c, :], b.astype(jnp.bfloat16), preferred_element_type=jnp.float32)
        for a, b, c in zip(exp_a, exp_b, heads)
    ]
    o_ref[...] = jnp.concatenate([m / d for m, d in zip(mixed, denominator)], axis=0).astype(o_ref.dtype)


def attend(keys_a, keys_b, queries_t, values_a, values_b):
    channels, total = queries_t.shape
    count = keys_a.shape[0]
    width = channels if total * count * channels <= 256 * 512 * 640 else 2 * HEAD_DIM
    key_spec = pl.BlockSpec((count, width), lambda j: (0, j))
    value_spec = pl.BlockSpec((width, count), lambda j: (j, 0))
    return pl.pallas_call(
        attention_kernel,
        grid=(channels // width,),
        in_specs=[key_spec, key_spec, pl.BlockSpec((width, total), lambda j: (j, 0)), value_spec, value_spec],
        out_specs=pl.BlockSpec((width, total), lambda j: (j, 0)),
        out_shape=jax.ShapeDtypeStruct((channels, total), jnp.bfloat16),
    )(keys_a, keys_b, queries_t, values_a, values_b)


def extended(array, axis, width):
    size, length = (lax.axis_size(axis), array.shape[0])
    up = [(i, i + 1) for i in range(size - 1)]
    down = [(j, i) for i, j in up]
    last = lax.slice_in_dim(array, length - width, length, axis=0)
    first = lax.slice_in_dim(array, 0, width, axis=0)
    before = lax.ppermute(last, axis, up)
    after = lax.ppermute(first, axis, down)
    return jnp.concatenate([before, array, after], axis=0)


def temporal_mix(padded, weights, count):
    result = jnp.zeros((count * padded.shape[1], padded.shape[2]), jnp.float32)
    for offset in range(3):
        window = padded[offset : offset + count].reshape(-1, padded.shape[2])
        result = result + jnp.dot(window, weights[offset], preferred_element_type=jnp.float32)
    return result


def gather_keyframes(frames, key_index, early):
    n_loc, rows, channels = frames.shape
    fsize = lax.axis_size("frame")
    rsize = lax.axis_size("row")
    me = lax.axis_index("frame")
    last = n_loc * fsize - 1
    other = key_index[0] + key_index[1] - last
    owner_a = other // n_loc
    slot_a = other % n_loc
    owner_b = fsize - 1
    half = rows // 2

    def halves(h):
        return lax.dynamic_slice_in_dim(frames, h * half, half, 1)

    own = halves(me % 2)
    got_a = jnp.where(
        me == owner_a, lax.dynamic_index_in_dim(own, slot_a, 0, keepdims=False), jnp.zeros_like(own[0])
    )
    got_b = own[n_loc - 1]
    for s in range(1, fsize):
        recv = lax.ppermute(halves((me + s) % 2), "frame", [(i, (i + s) % fsize) for i in range(fsize)])
        source = (me - s) % fsize
        got_a = jnp.where(source == owner_a, lax.dynamic_index_in_dim(recv, slot_a, 0, keepdims=False), got_a)
        got_b = jnp.where(source == owner_b, recv[n_loc - 1], got_b)
    piece = jnp.stack([got_a, got_b])
    piece, early = lax.optimization_barrier((piece, early))
    pieces = [piece]
    for s in range(1, rsize):
        pieces.append(lax.ppermute(piece, "row", [(i, (i + s) % rsize) for i in range(rsize)]))
    mine = jnp.stack(pieces).reshape(-1, channels)
    sibling = lax.ppermute(mine, "frame", [(i, i ^ 1) for i in range(fsize)])
    return mine, sibling


def shards(frames, key_index, w_query, w_keyval, w_out, norm_gain, w_first, w_second):
    frame_count, row_count, channels = frames.shape
    assert frame_count >= 2
    flattened = frames.reshape(-1, channels)
    queries_t = lax.dot_general(w_query, flattened, (((0,), (1,)), ((), ())), preferred_element_type=jnp.float32)
    queries_t = (queries_t * HEAD_DIM ** (-0.5)).astype(jnp.bfloat16)
    mine, sibling = gather_keyframes(frames, key_index, queries_t)

    def project(tokens):
        keys = jnp.dot(tokens, w_keyval[:, :channels], preferred_element_type=jnp.float32).astype(jnp.bfloat16)
        values_t = lax.dot_general(
            w_keyval[:, channels:], tokens, (((0,), (1,)), ((), ())), preferred_element_type=jnp.float32
        ).astype(jnp.bfloat16)
        return keys, values_t

    keys_mine, values_mine = project(mine)
    keys_sib, values_sib = project(sibling)
    attended_t = attend(keys_mine, keys_sib, queries_t, values_mine, values_sib)
    residual = flattened.astype(jnp.float32) + lax.dot_general(
        attended_t, w_out, (((0,), (0,)), ((), ())), preferred_element_type=jnp.float32
    )
    mean_square = jnp.mean(residual * residual, axis=-1, keepdims=True)
    normed = (residual * lax.rsqrt(mean_square + 1e-06) * norm_gain).astype(jnp.bfloat16)
    normed = normed.reshape(frame_count, row_count, channels)
    padded = extended(normed, "frame", 2)
    hidden = jax.nn.silu(temporal_mix(padded, w_first, frame_count + 2)).astype(jnp.bfloat16)
    hidden = hidden.reshape(frame_count + 2, row_count, channels)
    me = lax.axis_index("frame")
    outside = jnp.zeros((1, row_count, channels), hidden.dtype)
    hidden = jnp.concatenate(
        [
            jnp.where(me == 0, outside, hidden[:1]),
            hidden[1:-1],
            jnp.where(me == lax.axis_size("frame") - 1, outside, hidden[-1:]),
        ],
        axis=0,
    )
    second = temporal_mix(hidden, w_second, frame_count)
    return (residual + second).astype(jnp.bfloat16).reshape(frame_count, row_count, channels)


def solution(mesh):
    return jax.shard_map(
        shards,
        mesh=mesh,
        in_specs=(P(("clips", "frame"), "row", None), P("clips"), P(), P(), P(), P(), P(), P()),
        out_specs=P(("clips", "frame"), "row", None),
        check_vma=False,
    )
```

```python
import jax
import jax.numpy as jnp
from jax import lax
from jax.experimental import pallas as pl
from jax.sharding import PartitionSpec as P

HEADS = 10
HEAD_DIM = 64


def attention_kernel(k_ref, qt_ref, vt_ref, o_ref):
    heads = [slice(h * HEAD_DIM, (h + 1) * HEAD_DIM) for h in range(qt_ref.shape[0] // HEAD_DIM)]
    scores = [jnp.dot(k_ref[:, c], qt_ref[c, :], preferred_element_type=jnp.float32) for c in heads]
    highest = [jnp.max(s, axis=0, keepdims=True) for s in scores]
    exponent = [jnp.exp(s - m) for s, m in zip(scores, highest)]
    denominator = [jnp.sum(e, axis=0, keepdims=True) for e in exponent]
    mixed = [
        jnp.dot(vt_ref[c, :], e.astype(jnp.bfloat16), preferred_element_type=jnp.float32)
        for e, c in zip(exponent, heads)
    ]
    o_ref[...] = jnp.concatenate([m / d for m, d in zip(mixed, denominator)], axis=0).astype(o_ref.dtype)


def attend(keys, queries_t, values_t):
    channels, total = queries_t.shape
    count = keys.shape[0]
    width = channels if total * count * channels <= 256 * 1024 * 640 else 2 * HEAD_DIM
    return pl.pallas_call(
        attention_kernel,
        grid=(channels // width,),
        in_specs=[
            pl.BlockSpec((count, width), lambda j: (0, j)),
            pl.BlockSpec((width, total), lambda j: (j, 0)),
            pl.BlockSpec((width, count), lambda j: (j, 0)),
        ],
        out_specs=pl.BlockSpec((width, total), lambda j: (j, 0)),
        out_shape=jax.ShapeDtypeStruct((channels, total), jnp.bfloat16),
    )(keys, queries_t, values_t)


def extended(array, axis, width):
    size, length = (lax.axis_size(axis), array.shape[0])
    up = [(i, i + 1) for i in range(size - 1)]
    down = [(j, i) for i, j in up]
    last = lax.slice_in_dim(array, length - width, length, axis=0)
    first = lax.slice_in_dim(array, 0, width, axis=0)
    before = lax.ppermute(last, axis, up)
    after = lax.ppermute(first, axis, down)
    return jnp.concatenate([before, array, after], axis=0)


def temporal_mix(padded, weights, count):
    result = jnp.zeros((count * padded.shape[1], padded.shape[2]), jnp.float32)
    for offset in range(3):
        window = padded[offset : offset + count].reshape(-1, padded.shape[2])
        result = result + jnp.dot(window, weights[offset], preferred_element_type=jnp.float32)
    return result


def gather_keyframes(frames, key_index, early):
    n_loc, rows, channels = frames.shape
    fsize = lax.axis_size("frame")
    rsize = lax.axis_size("row")
    me = lax.axis_index("frame")
    last = n_loc * fsize - 1
    other = key_index[0] + key_index[1] - last
    owner_a = other // n_loc
    slot_a = other % n_loc
    owner_b = fsize - 1
    half = rows // 2

    def halves(h):
        return lax.dynamic_slice_in_dim(frames, h * half, half, 1)

    own = halves(me % 2)
    got_a = jnp.where(
        me == owner_a, lax.dynamic_index_in_dim(own, slot_a, 0, keepdims=False), jnp.zeros_like(own[0])
    )
    got_b = own[n_loc - 1]
    for s in range(1, fsize):
        recv = lax.ppermute(halves((me + s) % 2), "frame", [(i, (i + s) % fsize) for i in range(fsize)])
        source = (me - s) % fsize
        got_a = jnp.where(source == owner_a, lax.dynamic_index_in_dim(recv, slot_a, 0, keepdims=False), got_a)
        got_b = jnp.where(source == owner_b, recv[n_loc - 1], got_b)
    piece = jnp.stack([got_a, got_b])
    piece, early = lax.optimization_barrier((piece, early))
    pieces = [piece]
    for s in range(1, rsize):
        pieces.append(lax.ppermute(piece, "row", [(i, (i + s) % rsize) for i in range(rsize)]))
    mine = jnp.stack(pieces).reshape(-1, channels)
    sibling = lax.ppermute(mine, "frame", [(i, i ^ 1) for i in range(fsize)])
    return mine, sibling


def shards(frames, key_index, w_query, w_keyval, w_out, norm_gain, w_first, w_second):
    frame_count, row_count, channels = frames.shape
    assert frame_count >= 2
    flattened = frames.reshape(-1, channels)
    queries_t = lax.dot_general(w_query, flattened, (((0,), (1,)), ((), ())), preferred_element_type=jnp.float32)
    queries_t = (queries_t * HEAD_DIM ** (-0.5)).astype(jnp.bfloat16)
    mine, sibling = gather_keyframes(frames, key_index, queries_t)

    def project(tokens):
        keys = jnp.dot(tokens, w_keyval[:, :channels], preferred_element_type=jnp.float32).astype(jnp.bfloat16)
        values_t = lax.dot_general(
            w_keyval[:, channels:], tokens, (((0,), (1,)), ((), ())), preferred_element_type=jnp.float32
        ).astype(jnp.bfloat16)
        return keys, values_t

    keys_mine, values_mine = project(mine)
    keys_sib, values_sib = project(sibling)
    keys = jnp.concatenate([keys_mine, keys_sib], axis=0)
    values_t = jnp.concatenate([values_mine, values_sib], axis=1)
    attended_t = attend(keys, queries_t, values_t)
    residual = flattened.astype(jnp.float32) + lax.dot_general(
        attended_t, w_out, (((0,), (0,)), ((), ())), preferred_element_type=jnp.float32
    )
    mean_square = jnp.mean(residual * residual, axis=-1, keepdims=True)
    normed = (residual * lax.rsqrt(mean_square + 1e-06) * norm_gain).astype(jnp.bfloat16)
    normed = normed.reshape(frame_count, row_count, channels)
    halo = extended(normed, "frame", 2)
    before, after = halo[:2], halo[-2:]
    flat_normed = normed.reshape(-1, channels)
    local = 0.0
    for tap in range(3):
        part = jnp.dot(flat_normed, w_first[tap], preferred_element_type=jnp.float32)
        part = part.reshape(frame_count, row_count, channels)
        local = local + jnp.pad(part, ((2 - tap, tap), (0, 0), (0, 0)))
    first_out = jnp.einsum("frc,fcd->rd", before, w_first[0:2], preferred_element_type=jnp.float32)
    second_out = jnp.dot(before[1], w_first[0], preferred_element_type=jnp.float32)
    last_but_one = jnp.dot(after[0], w_first[2], preferred_element_type=jnp.float32)
    last_out = jnp.einsum("frc,fcd->rd", after, w_first[1:3], preferred_element_type=jnp.float32)
    halo_part = jnp.concatenate(
        [
            jnp.stack([first_out, second_out]),
            jnp.zeros((frame_count - 2, row_count, channels), jnp.float32),
            jnp.stack([last_but_one, last_out]),
        ],
        axis=0,
    )
    hidden = jax.nn.silu(local + halo_part).astype(jnp.bfloat16)
    hidden = hidden.reshape(frame_count + 2, row_count, channels)
    me = lax.axis_index("frame")
    outside = jnp.zeros((1, row_count, channels), hidden.dtype)
    hidden = jnp.concatenate(
        [
            jnp.where(me == 0, outside, hidden[:1]),
            hidden[1:-1],
            jnp.where(me == lax.axis_size("frame") - 1, outside, hidden[-1:]),
        ],
        axis=0,
    )
    second = temporal_mix(hidden, w_second, frame_count)
    return (residual + second).astype(jnp.bfloat16).reshape(frame_count, row_count, channels)


def solution(mesh):
    return jax.shard_map(
        shards,
        mesh=mesh,
        in_specs=(P(("clips", "frame"), "row", None), P("clips"), P(), P(), P(), P(), P(), P()),
        out_specs=P(("clips", "frame"), "row", None),
        check_vma=False,
    )
```

```python
import jax
import jax.numpy as jnp
from jax import lax
from jax.experimental import pallas as pl
from jax.sharding import PartitionSpec as P

HEADS = 10
HEAD_DIM = 64


def _heads(ref):
    return [slice(h * HEAD_DIM, (h + 1) * HEAD_DIM) for h in range(ref.shape[0] // HEAD_DIM)]


def first_chunk_kernel(k_ref, qt_ref, vt_ref, m_ref, l_ref, acc_ref):
    heads = _heads(qt_ref)
    scores = [jnp.dot(k_ref[:, c], qt_ref[c, :], preferred_element_type=jnp.float32) for c in heads]
    highest = [jnp.max(s, axis=0, keepdims=True) for s in scores]
    exponent = [jnp.exp(s - m) for s, m in zip(scores, highest)]
    for c, m, e in zip(heads, highest, exponent):
        mixed = jnp.dot(vt_ref[c, :], e.astype(jnp.bfloat16), preferred_element_type=jnp.float32)
        m_ref[c, :] = jnp.broadcast_to(m, mixed.shape)
        l_ref[c, :] = jnp.broadcast_to(jnp.sum(e, axis=0, keepdims=True), mixed.shape)
        acc_ref[c, :] = mixed


def last_chunk_kernel(k_ref, qt_ref, vt_ref, m_ref, l_ref, acc_ref, o_ref):
    heads = _heads(qt_ref)
    scores = [jnp.dot(k_ref[:, c], qt_ref[c, :], preferred_element_type=jnp.float32) for c in heads]
    before = [jnp.max(m_ref[c, :], axis=0, keepdims=True) for c in heads]
    highest = [jnp.maximum(b, jnp.max(s, axis=0, keepdims=True)) for b, s in zip(before, scores)]
    kept = [jnp.exp(b - m) for b, m in zip(before, highest)]
    exponent = [jnp.exp(s - m) for s, m in zip(scores, highest)]
    outs = []
    for c, k, e in zip(heads, kept, exponent):
        total = jnp.max(l_ref[c, :], axis=0, keepdims=True) * k + jnp.sum(e, axis=0, keepdims=True)
        mixed = acc_ref[c, :] * k + jnp.dot(vt_ref[c, :], e.astype(jnp.bfloat16), preferred_element_type=jnp.float32)
        outs.append(mixed / total)
    o_ref[...] = jnp.concatenate(outs, axis=0).astype(o_ref.dtype)


def _attention_specs(channels, total, count):
    width = channels if total * count * channels <= 256 * 1024 * 640 else 2 * HEAD_DIM
    rows = pl.BlockSpec((width, total), lambda j: (j, 0))
    keys = pl.BlockSpec((count, width), lambda j: (0, j))
    values = pl.BlockSpec((width, count), lambda j: (j, 0))
    return channels // width, rows, keys, values


def attend_first(keys, queries_t, values_t):
    channels, total = queries_t.shape
    steps, rows, key_spec, value_spec = _attention_specs(channels, total, keys.shape[0])
    state = jax.ShapeDtypeStruct((channels, total), jnp.float32)
    return pl.pallas_call(
        first_chunk_kernel,
        grid=(steps,),
        in_specs=[key_spec, rows, value_spec],
        out_specs=[rows, rows, rows],
        out_shape=[state, state, state],
    )(keys, queries_t, values_t)


def attend_last(keys, queries_t, values_t, state):
    channels, total = queries_t.shape
    steps, rows, key_spec, value_spec = _attention_specs(channels, total, keys.shape[0])
    return pl.pallas_call(
        last_chunk_kernel,
        grid=(steps,),
        in_specs=[key_spec, rows, value_spec, rows, rows, rows],
        out_specs=rows,
        out_shape=jax.ShapeDtypeStruct((channels, total), jnp.bfloat16),
    )(keys, queries_t, values_t, *state)


def extended(array, axis, width):
    size, length = (lax.axis_size(axis), array.shape[0])
    up = [(i, i + 1) for i in range(size - 1)]
    down = [(j, i) for i, j in up]
    last = lax.slice_in_dim(array, length - width, length, axis=0)
    first = lax.slice_in_dim(array, 0, width, axis=0)
    before = lax.ppermute(last, axis, up)
    after = lax.ppermute(first, axis, down)
    return jnp.concatenate([before, array, after], axis=0)


def temporal_mix(padded, weights, count):
    result = jnp.zeros((count * padded.shape[1], padded.shape[2]), jnp.float32)
    for offset in range(3):
        window = padded[offset : offset + count].reshape(-1, padded.shape[2])
        result = result + jnp.dot(window, weights[offset], preferred_element_type=jnp.float32)
    return result


def gather_keyframes(frames, key_index, early):
    n_loc, rows, channels = frames.shape
    fsize = lax.axis_size("frame")
    rsize = lax.axis_size("row")
    me = lax.axis_index("frame")
    last = n_loc * fsize - 1
    other = key_index[0] + key_index[1] - last
    owner_a = other // n_loc
    slot_a = other % n_loc
    owner_b = fsize - 1
    half = rows // 2

    def halves(h):
        return lax.dynamic_slice_in_dim(frames, h * half, half, 1)

    own = halves(me % 2)
    got_a = jnp.where(
        me == owner_a, lax.dynamic_index_in_dim(own, slot_a, 0, keepdims=False), jnp.zeros_like(own[0])
    )
    got_b = own[n_loc - 1]
    for s in range(1, fsize):
        recv = lax.ppermute(halves((me + s) % 2), "frame", [(i, (i + s) % fsize) for i in range(fsize)])
        source = (me - s) % fsize
        got_a = jnp.where(source == owner_a, lax.dynamic_index_in_dim(recv, slot_a, 0, keepdims=False), got_a)
        got_b = jnp.where(source == owner_b, recv[n_loc - 1], got_b)
    piece = jnp.stack([got_a, got_b])
    piece, early = lax.optimization_barrier((piece, early))
    swap = [(i, i ^ 1) for i in range(fsize)]
    own_row = jnp.concatenate([piece, lax.ppermute(piece, "frame", swap)], axis=0).reshape(-1, channels)
    pieces = []
    for s in range(1, rsize):
        pieces.append(lax.ppermute(piece, "row", [(i, (i + s) % rsize) for i in range(rsize)]))
    return own_row, pieces


def shards(frames, key_index, w_query, w_keyval, w_out, norm_gain, w_first, w_second):
    frame_count, row_count, channels = frames.shape
    assert frame_count >= 2
    flattened = frames.reshape(-1, channels)
    queries_t = lax.dot_general(w_query, flattened, (((0,), (1,)), ((), ())), preferred_element_type=jnp.float32)
    queries_t = (queries_t * HEAD_DIM ** (-0.5)).astype(jnp.bfloat16)
    own_row, pieces = gather_keyframes(frames, key_index, queries_t)

    def project(tokens):
        keys = jnp.dot(tokens, w_keyval[:, :channels], preferred_element_type=jnp.float32).astype(jnp.bfloat16)
        values_t = lax.dot_general(
            w_keyval[:, channels:], tokens, (((0,), (1,)), ((), ())), preferred_element_type=jnp.float32
        ).astype(jnp.bfloat16)
        return keys, values_t

    state = attend_first(project(own_row)[0], queries_t, project(own_row)[1])
    pieces, state = lax.optimization_barrier((pieces, state))
    mine = jnp.stack(pieces).reshape(-1, channels)
    sibling = lax.ppermute(mine, "frame", [(i, i ^ 1) for i in range(lax.axis_size("frame"))])
    keys_mine, values_mine = project(mine)
    keys_sib, values_sib = project(sibling)
    keys = jnp.concatenate([keys_mine, keys_sib], axis=0)
    values_t = jnp.concatenate([values_mine, values_sib], axis=1)
    attended_t = attend_last(keys, queries_t, values_t, state)
    residual = flattened.astype(jnp.float32) + lax.dot_general(
        attended_t, w_out, (((0,), (0,)), ((), ())), preferred_element_type=jnp.float32
    )
    mean_square = jnp.mean(residual * residual, axis=-1, keepdims=True)
    normed = (residual * lax.rsqrt(mean_square + 1e-06) * norm_gain).astype(jnp.bfloat16)
    normed = normed.reshape(frame_count, row_count, channels)
    padded = extended(normed, "frame", 2)
    hidden = jax.nn.silu(temporal_mix(padded, w_first, frame_count + 2)).astype(jnp.bfloat16)
    hidden = hidden.reshape(frame_count + 2, row_count, channels)
    me = lax.axis_index("frame")
    outside = jnp.zeros((1, row_count, channels), hidden.dtype)
    hidden = jnp.concatenate(
        [
            jnp.where(me == 0, outside, hidden[:1]),
            hidden[1:-1],
            jnp.where(me == lax.axis_size("frame") - 1, outside, hidden[-1:]),
        ],
        axis=0,
    )
    second = temporal_mix(hidden, w_second, frame_count)
    return (residual + second).astype(jnp.bfloat16).reshape(frame_count, row_count, channels)


def solution(mesh):
    return jax.shard_map(
        shards,
        mesh=mesh,
        in_specs=(P(("clips", "frame"), "row", None), P("clips"), P(), P(), P(), P(), P(), P()),
        out_specs=P(("clips", "frame"), "row", None),
        check_vma=False,
    )
```

```python
import jax
import jax.numpy as jnp
from jax import lax
from jax.experimental import pallas as pl
from jax.sharding import PartitionSpec as P

HEADS = 10
HEAD_DIM = 64


def attention_kernel(k_ref, qt_ref, vt_ref, o_ref):
    heads = [slice(h * HEAD_DIM, (h + 1) * HEAD_DIM) for h in range(qt_ref.shape[0] // HEAD_DIM)]
    scores = [jnp.dot(k_ref[:, c], qt_ref[c, :], preferred_element_type=jnp.float32) for c in heads]
    highest = [jnp.max(s, axis=0, keepdims=True) for s in scores]
    exponent = [jnp.exp(s - m) for s, m in zip(scores, highest)]
    denominator = [jnp.sum(e, axis=0, keepdims=True) for e in exponent]
    mixed = [
        jnp.dot(vt_ref[c, :], e.astype(jnp.bfloat16), preferred_element_type=jnp.float32)
        for e, c in zip(exponent, heads)
    ]
    o_ref[...] = jnp.concatenate([m / d for m, d in zip(mixed, denominator)], axis=0).astype(o_ref.dtype)


def attend(keys, queries_t, values_t):
    channels, total = queries_t.shape
    count = keys.shape[0]
    width = channels if total * count * channels <= 256 * 1024 * 640 else 2 * HEAD_DIM
    return pl.pallas_call(
        attention_kernel,
        grid=(channels // width,),
        in_specs=[
            pl.BlockSpec((count, width), lambda j: (0, j)),
            pl.BlockSpec((width, total), lambda j: (j, 0)),
            pl.BlockSpec((width, count), lambda j: (j, 0)),
        ],
        out_specs=pl.BlockSpec((width, total), lambda j: (j, 0)),
        out_shape=jax.ShapeDtypeStruct((channels, total), jnp.bfloat16),
    )(keys, queries_t, values_t)


def attention_block_kernel(k_ref, qt_ref, vt_ref, x_ref, w_ref, g_ref, r_ref, n_ref):
    heads = [slice(h * HEAD_DIM, (h + 1) * HEAD_DIM) for h in range(qt_ref.shape[0] // HEAD_DIM)]
    scores = [jnp.dot(k_ref[:, c], qt_ref[c, :], preferred_element_type=jnp.float32) for c in heads]
    highest = [jnp.max(s, axis=0, keepdims=True) for s in scores]
    exponent = [jnp.exp(s - m) for s, m in zip(scores, highest)]
    denominator = [jnp.sum(e, axis=0, keepdims=True) for e in exponent]
    mixed = [
        jnp.dot(vt_ref[c, :], e.astype(jnp.bfloat16), preferred_element_type=jnp.float32)
        for e, c in zip(exponent, heads)
    ]
    attended_t = jnp.concatenate([m / d for m, d in zip(mixed, denominator)], axis=0).astype(jnp.bfloat16)
    projected = lax.dot_general(attended_t, w_ref[...], (((0,), (0,)), ((), ())), preferred_element_type=jnp.float32)
    residual = x_ref[...].astype(jnp.float32) + projected
    mean_square = jnp.mean(residual * residual, axis=1, keepdims=True)
    r_ref[...] = residual
    n_ref[...] = (residual * lax.rsqrt(mean_square + 1e-06) * g_ref[...]).astype(n_ref.dtype)


def attention_block(keys, queries_t, values_t, tokens, w_out, norm_gain):
    total, channels = tokens.shape
    return pl.pallas_call(
        attention_block_kernel,
        out_shape=[
            jax.ShapeDtypeStruct((total, channels), jnp.float32),
            jax.ShapeDtypeStruct((total, channels), jnp.bfloat16),
        ],
    )(keys, queries_t, values_t, tokens, w_out, norm_gain.reshape(1, channels))


def extended(array, axis, width):
    size, length = (lax.axis_size(axis), array.shape[0])
    up = [(i, i + 1) for i in range(size - 1)]
    down = [(j, i) for i, j in up]
    last = lax.slice_in_dim(array, length - width, length, axis=0)
    first = lax.slice_in_dim(array, 0, width, axis=0)
    before = lax.ppermute(last, axis, up)
    after = lax.ppermute(first, axis, down)
    return jnp.concatenate([before, array, after], axis=0)


def temporal_mix(padded, weights, count):
    result = jnp.zeros((count * padded.shape[1], padded.shape[2]), jnp.float32)
    for offset in range(3):
        window = padded[offset : offset + count].reshape(-1, padded.shape[2])
        result = result + jnp.dot(window, weights[offset], preferred_element_type=jnp.float32)
    return result


def gather_keyframes(frames, key_index, early):
    n_loc, rows, channels = frames.shape
    fsize = lax.axis_size("frame")
    rsize = lax.axis_size("row")
    me = lax.axis_index("frame")
    last = n_loc * fsize - 1
    other = key_index[0] + key_index[1] - last
    owner_a = other // n_loc
    slot_a = other % n_loc
    owner_b = fsize - 1
    half = rows // 2

    def halves(h):
        return lax.dynamic_slice_in_dim(frames, h * half, half, 1)

    own = halves(me % 2)
    got_a = jnp.where(
        me == owner_a, lax.dynamic_index_in_dim(own, slot_a, 0, keepdims=False), jnp.zeros_like(own[0])
    )
    got_b = own[n_loc - 1]
    for s in range(1, fsize):
        recv = lax.ppermute(halves((me + s) % 2), "frame", [(i, (i + s) % fsize) for i in range(fsize)])
        source = (me - s) % fsize
        got_a = jnp.where(source == owner_a, lax.dynamic_index_in_dim(recv, slot_a, 0, keepdims=False), got_a)
        got_b = jnp.where(source == owner_b, recv[n_loc - 1], got_b)
    piece = jnp.stack([got_a, got_b])
    piece, early = lax.optimization_barrier((piece, early))
    pieces = [piece]
    for s in range(1, rsize):
        pieces.append(lax.ppermute(piece, "row", [(i, (i + s) % rsize) for i in range(rsize)]))
    mine = jnp.stack(pieces).reshape(-1, channels)
    sibling = lax.ppermute(mine, "frame", [(i, i ^ 1) for i in range(fsize)])
    return mine, sibling


def query_total_fits(queries_t, keys):
    channels, total = queries_t.shape
    return total * keys.shape[0] * channels <= 256 * 1024 * 640


def shards(frames, key_index, w_query, w_keyval, w_out, norm_gain, w_first, w_second):
    frame_count, row_count, channels = frames.shape
    assert frame_count >= 2
    flattened = frames.reshape(-1, channels)
    queries_t = lax.dot_general(w_query, flattened, (((0,), (1,)), ((), ())), preferred_element_type=jnp.float32)
    queries_t = (queries_t * HEAD_DIM ** (-0.5)).astype(jnp.bfloat16)
    mine, sibling = gather_keyframes(frames, key_index, queries_t)

    def project(tokens):
        keys = jnp.dot(tokens, w_keyval[:, :channels], preferred_element_type=jnp.float32).astype(jnp.bfloat16)
        values_t = lax.dot_general(
            w_keyval[:, channels:], tokens, (((0,), (1,)), ((), ())), preferred_element_type=jnp.float32
        ).astype(jnp.bfloat16)
        return keys, values_t

    keys_mine, values_mine = project(mine)
    keys_sib, values_sib = project(sibling)
    keys = jnp.concatenate([keys_mine, keys_sib], axis=0)
    values_t = jnp.concatenate([values_mine, values_sib], axis=1)
    if query_total_fits(queries_t, keys):
        residual, normed = attention_block(keys, queries_t, values_t, flattened, w_out, norm_gain)
    else:
        attended_t = attend(keys, queries_t, values_t)
        residual = flattened.astype(jnp.float32) + lax.dot_general(
            attended_t, w_out, (((0,), (0,)), ((), ())), preferred_element_type=jnp.float32
        )
        mean_square = jnp.mean(residual * residual, axis=-1, keepdims=True)
        normed = (residual * lax.rsqrt(mean_square + 1e-06) * norm_gain).astype(jnp.bfloat16)
    normed = normed.reshape(frame_count, row_count, channels)
    padded = extended(normed, "frame", 2)
    hidden = jax.nn.silu(temporal_mix(padded, w_first, frame_count + 2)).astype(jnp.bfloat16)
    hidden = hidden.reshape(frame_count + 2, row_count, channels)
    me = lax.axis_index("frame")
    outside = jnp.zeros((1, row_count, channels), hidden.dtype)
    hidden = jnp.concatenate(
        [
            jnp.where(me == 0, outside, hidden[:1]),
            hidden[1:-1],
            jnp.where(me == lax.axis_size("frame") - 1, outside, hidden[-1:]),
        ],
        axis=0,
    )
    second = temporal_mix(hidden, w_second, frame_count)
    return (residual + second).astype(jnp.bfloat16).reshape(frame_count, row_count, channels)


def solution(mesh):
    return jax.shard_map(
        shards,
        mesh=mesh,
        in_specs=(P(("clips", "frame"), "row", None), P("clips"), P(), P(), P(), P(), P(), P()),
        out_specs=P(("clips", "frame"), "row", None),
        check_vma=False,
    )
```

```python
import jax
import jax.numpy as jnp
from jax import lax
from jax.experimental import pallas as pl
from jax.sharding import PartitionSpec as P

HEADS = 10
HEAD_DIM = 64


def attention_kernel(k_ref, qt_ref, vt_ref, o_ref):
    heads = [slice(h * HEAD_DIM, (h + 1) * HEAD_DIM) for h in range(qt_ref.shape[0] // HEAD_DIM)]
    scores = [jnp.dot(k_ref[:, c], qt_ref[c, :], preferred_element_type=jnp.float32) for c in heads]
    highest = [jnp.max(s, axis=0, keepdims=True) for s in scores]
    exponent = [jnp.exp(s - m) for s, m in zip(scores, highest)]
    denominator = [jnp.sum(e, axis=0, keepdims=True) for e in exponent]
    mixed = [
        jnp.dot(vt_ref[c, :], e.astype(jnp.bfloat16), preferred_element_type=jnp.float32)
        for e, c in zip(exponent, heads)
    ]
    o_ref[...] = jnp.concatenate([m / d for m, d in zip(mixed, denominator)], axis=0).astype(o_ref.dtype)


def attend(keys, queries_t, values_t):
    channels, total = queries_t.shape
    count = keys.shape[0]
    width = channels if total * count * channels <= 256 * 1024 * 640 else 2 * HEAD_DIM
    return pl.pallas_call(
        attention_kernel,
        grid=(channels // width,),
        in_specs=[
            pl.BlockSpec((count, width), lambda j: (0, j)),
            pl.BlockSpec((width, total), lambda j: (j, 0)),
            pl.BlockSpec((width, count), lambda j: (j, 0)),
        ],
        out_specs=pl.BlockSpec((width, total), lambda j: (j, 0)),
        out_shape=jax.ShapeDtypeStruct((channels, total), jnp.bfloat16),
    )(keys, queries_t, values_t)


def extended(array, axis, width):
    size, length = (lax.axis_size(axis), array.shape[0])
    up = [(i, i + 1) for i in range(size - 1)]
    down = [(j, i) for i, j in up]
    last = lax.slice_in_dim(array, length - width, length, axis=0)
    first = lax.slice_in_dim(array, 0, width, axis=0)
    before = lax.ppermute(last, axis, up)
    after = lax.ppermute(first, axis, down)
    return jnp.concatenate([before, array, after], axis=0)


def temporal_mix(padded, weights, count):
    result = jnp.zeros((count * padded.shape[1], padded.shape[2]), jnp.float32)
    for offset in range(3):
        window = padded[offset : offset + count].reshape(-1, padded.shape[2])
        result = result + jnp.dot(window, weights[offset], preferred_element_type=jnp.float32)
    return result


def gather_keyframes(frames, key_index, early):
    n_loc, rows, channels = frames.shape
    fsize = lax.axis_size("frame")
    rsize = lax.axis_size("row")
    me = lax.axis_index("frame")
    last = n_loc * fsize - 1
    other = key_index[0] + key_index[1] - last
    owner_a = other // n_loc
    slot_a = other % n_loc
    owner_b = fsize - 1
    half = rows // 2

    def halves(h):
        return lax.dynamic_slice_in_dim(frames, h * half, half, 1)

    own = halves(me % 2)
    got_a = jnp.where(
        me == owner_a, lax.dynamic_index_in_dim(own, slot_a, 0, keepdims=False), jnp.zeros_like(own[0])
    )
    got_b = own[n_loc - 1]
    for s in range(1, fsize):
        recv = lax.ppermute(halves((me + s) % 2), "frame", [(i, (i + s) % fsize) for i in range(fsize)])
        source = (me - s) % fsize
        got_a = jnp.where(source == owner_a, lax.dynamic_index_in_dim(recv, slot_a, 0, keepdims=False), got_a)
        got_b = jnp.where(source == owner_b, recv[n_loc - 1], got_b)
    piece = jnp.stack([got_a, got_b])
    piece, early = lax.optimization_barrier((piece, early))
    pieces = []
    for s in range(1, rsize):
        pieces.append(lax.ppermute(piece, "row", [(i, (i + s) % rsize) for i in range(rsize)]))
    own_row = jnp.concatenate([piece, lax.ppermute(piece, "frame", [(i, i ^ 1) for i in range(fsize)])], axis=0)
    return own_row.reshape(-1, channels), pieces


def shards(frames, key_index, w_query, w_keyval, w_out, norm_gain, w_first, w_second):
    frame_count, row_count, channels = frames.shape
    assert frame_count >= 2
    flattened = frames.reshape(-1, channels)
    queries_t = lax.dot_general(w_query, flattened, (((0,), (1,)), ((), ())), preferred_element_type=jnp.float32)
    queries_t = (queries_t * HEAD_DIM ** (-0.5)).astype(jnp.bfloat16)
    own_row, pieces = gather_keyframes(frames, key_index, queries_t)

    def project(tokens):
        keys = jnp.dot(tokens, w_keyval[:, :channels], preferred_element_type=jnp.float32).astype(jnp.bfloat16)
        values_t = lax.dot_general(
            w_keyval[:, channels:], tokens, (((0,), (1,)), ((), ())), preferred_element_type=jnp.float32
        ).astype(jnp.bfloat16)
        return keys, values_t

    keys_own, values_own = project(own_row)
    pieces, keys_own, values_own = lax.optimization_barrier((pieces, keys_own, values_own))
    mine = jnp.stack(pieces).reshape(-1, channels)
    sibling = lax.ppermute(mine, "frame", [(i, i ^ 1) for i in range(lax.axis_size("frame"))])
    keys_mine, values_mine = project(mine)
    keys_sib, values_sib = project(sibling)
    keys = jnp.concatenate([keys_own, keys_mine, keys_sib], axis=0)
    values_t = jnp.concatenate([values_own, values_mine, values_sib], axis=1)
    attended_t = attend(keys, queries_t, values_t)
    residual = flattened.astype(jnp.float32) + lax.dot_general(
        attended_t, w_out, (((0,), (0,)), ((), ())), preferred_element_type=jnp.float32
    )
    mean_square = jnp.mean(residual * residual, axis=-1, keepdims=True)
    normed = (residual * lax.rsqrt(mean_square + 1e-06) * norm_gain).astype(jnp.bfloat16)
    normed = normed.reshape(frame_count, row_count, channels)
    padded = extended(normed, "frame", 2)
    hidden = jax.nn.silu(temporal_mix(padded, w_first, frame_count + 2)).astype(jnp.bfloat16)
    hidden = hidden.reshape(frame_count + 2, row_count, channels)
    me = lax.axis_index("frame")
    outside = jnp.zeros((1, row_count, channels), hidden.dtype)
    hidden = jnp.concatenate(
        [
            jnp.where(me == 0, outside, hidden[:1]),
            hidden[1:-1],
            jnp.where(me == lax.axis_size("frame") - 1, outside, hidden[-1:]),
        ],
        axis=0,
    )
    second = temporal_mix(hidden, w_second, frame_count)
    return (residual + second).astype(jnp.bfloat16).reshape(frame_count, row_count, channels)


def solution(mesh):
    return jax.shard_map(
        shards,
        mesh=mesh,
        in_specs=(P(("clips", "frame"), "row", None), P("clips"), P(), P(), P(), P(), P(), P()),
        out_specs=P(("clips", "frame"), "row", None),
        check_vma=False,
    )
```

```python
import jax
import jax.numpy as jnp
from jax import lax
from jax.experimental import pallas as pl
from jax.sharding import PartitionSpec as P

HEADS = 10
HEAD_DIM = 64


def attention_kernel(k_ref, qt_ref, vt_ref, o_ref):
    heads = [slice(h * HEAD_DIM, (h + 1) * HEAD_DIM) for h in range(qt_ref.shape[0] // HEAD_DIM)]
    scores = [jnp.dot(k_ref[:, c], qt_ref[c, :], preferred_element_type=jnp.float32) for c in heads]
    highest = [jnp.max(s, axis=0, keepdims=True) for s in scores]
    exponent = [jnp.exp(s - m) for s, m in zip(scores, highest)]
    denominator = [jnp.sum(e, axis=0, keepdims=True) for e in exponent]
    mixed = [
        jnp.dot(vt_ref[c, :], e.astype(jnp.bfloat16), preferred_element_type=jnp.float32)
        for e, c in zip(exponent, heads)
    ]
    o_ref[...] = jnp.concatenate([m / d for m, d in zip(mixed, denominator)], axis=0).astype(o_ref.dtype)


def attend(keys, queries_t, values_t):
    channels, total = queries_t.shape
    count = keys.shape[0]
    width = channels if total * count * channels <= 256 * 1024 * 640 else 2 * HEAD_DIM
    return pl.pallas_call(
        attention_kernel,
        grid=(channels // width,),
        in_specs=[
            pl.BlockSpec((count, width), lambda j: (0, j)),
            pl.BlockSpec((width, total), lambda j: (j, 0)),
            pl.BlockSpec((width, count), lambda j: (j, 0)),
        ],
        out_specs=pl.BlockSpec((width, total), lambda j: (j, 0)),
        out_shape=jax.ShapeDtypeStruct((channels, total), jnp.bfloat16),
    )(keys, queries_t, values_t)


def extended(array, axis, width):
    size, length = (lax.axis_size(axis), array.shape[0])
    up = [(i, i + 1) for i in range(size - 1)]
    down = [(j, i) for i, j in up]
    last = lax.slice_in_dim(array, length - width, length, axis=0)
    first = lax.slice_in_dim(array, 0, width, axis=0)
    before = lax.ppermute(last, axis, up)
    after = lax.ppermute(first, axis, down)
    return jnp.concatenate([before, array, after], axis=0)


def temporal_mix(padded, weights, count):
    result = jnp.zeros((count * padded.shape[1], padded.shape[2]), jnp.float32)
    for offset in range(3):
        window = padded[offset : offset + count].reshape(-1, padded.shape[2])
        result = result + jnp.dot(window, weights[offset], preferred_element_type=jnp.float32)
    return result


def gather_keyframes(frames, key_index, early):
    n_loc, rows, channels = frames.shape
    fsize = lax.axis_size("frame")
    rsize = lax.axis_size("row")
    me = lax.axis_index("frame")
    last = n_loc * fsize - 1
    other = key_index[0] + key_index[1] - last
    owner_a = other // n_loc
    slot_a = other % n_loc
    owner_b = fsize - 1
    half = rows // 2

    def halves(h):
        return lax.dynamic_slice_in_dim(frames, h * half, half, 1)

    own = halves(me % 2)
    got_a = jnp.where(
        me == owner_a, lax.dynamic_index_in_dim(own, slot_a, 0, keepdims=False), jnp.zeros_like(own[0])
    )
    got_b = own[n_loc - 1]
    for s in range(1, fsize):
        recv = lax.ppermute(halves((me + s) % 2), "frame", [(i, (i + s) % fsize) for i in range(fsize)])
        source = (me - s) % fsize
        got_a = jnp.where(source == owner_a, lax.dynamic_index_in_dim(recv, slot_a, 0, keepdims=False), got_a)
        got_b = jnp.where(source == owner_b, recv[n_loc - 1], got_b)
    piece = jnp.stack([got_a, got_b])
    piece, early = lax.optimization_barrier((piece, early))
    if rsize & (rsize - 1) == 0:
        gathered = piece[None]
        stride = 1
        while stride < rsize:
            moved = lax.ppermute(gathered, "row", [(i, (i + stride) % rsize) for i in range(rsize)])
            gathered = jnp.concatenate([gathered, moved], axis=0)
            stride *= 2
        mine = gathered.reshape(-1, channels)
    else:
        pieces = [piece]
        for s in range(1, rsize):
            pieces.append(lax.ppermute(piece, "row", [(i, (i + s) % rsize) for i in range(rsize)]))
        mine = jnp.stack(pieces).reshape(-1, channels)
    sibling = lax.ppermute(mine, "frame", [(i, i ^ 1) for i in range(fsize)])
    return mine, sibling


def shards(frames, key_index, w_query, w_keyval, w_out, norm_gain, w_first, w_second):
    frame_count, row_count, channels = frames.shape
    assert frame_count >= 2
    flattened = frames.reshape(-1, channels)
    queries_t = lax.dot_general(w_query, flattened, (((0,), (1,)), ((), ())), preferred_element_type=jnp.float32)
    queries_t = (queries_t * HEAD_DIM ** (-0.5)).astype(jnp.bfloat16)
    mine, sibling = gather_keyframes(frames, key_index, queries_t)

    def project(tokens):
        keys = jnp.dot(tokens, w_keyval[:, :channels], preferred_element_type=jnp.float32).astype(jnp.bfloat16)
        values_t = lax.dot_general(
            w_keyval[:, channels:], tokens, (((0,), (1,)), ((), ())), preferred_element_type=jnp.float32
        ).astype(jnp.bfloat16)
        return keys, values_t

    keys_mine, values_mine = project(mine)
    keys_sib, values_sib = project(sibling)
    keys = jnp.concatenate([keys_mine, keys_sib], axis=0)
    values_t = jnp.concatenate([values_mine, values_sib], axis=1)
    attended_t = attend(keys, queries_t, values_t)
    residual = flattened.astype(jnp.float32) + lax.dot_general(
        attended_t, w_out, (((0,), (0,)), ((), ())), preferred_element_type=jnp.float32
    )
    mean_square = jnp.mean(residual * residual, axis=-1, keepdims=True)
    normed = (residual * lax.rsqrt(mean_square + 1e-06) * norm_gain).astype(jnp.bfloat16)
    normed = normed.reshape(frame_count, row_count, channels)
    padded = extended(normed, "frame", 2)
    hidden = jax.nn.silu(temporal_mix(padded, w_first, frame_count + 2)).astype(jnp.bfloat16)
    hidden = hidden.reshape(frame_count + 2, row_count, channels)
    me = lax.axis_index("frame")
    outside = jnp.zeros((1, row_count, channels), hidden.dtype)
    hidden = jnp.concatenate(
        [
            jnp.where(me == 0, outside, hidden[:1]),
            hidden[1:-1],
            jnp.where(me == lax.axis_size("frame") - 1, outside, hidden[-1:]),
        ],
        axis=0,
    )
    second = temporal_mix(hidden, w_second, frame_count)
    return (residual + second).astype(jnp.bfloat16).reshape(frame_count, row_count, channels)


def solution(mesh):
    return jax.shard_map(
        shards,
        mesh=mesh,
        in_specs=(P(("clips", "frame"), "row", None), P("clips"), P(), P(), P(), P(), P(), P()),
        out_specs=P(("clips", "frame"), "row", None),
        check_vma=False,
    )
```

```python
import jax
import jax.numpy as jnp
from jax import lax
from jax.experimental import pallas as pl
from jax.sharding import PartitionSpec as P

HEADS = 10
HEAD_DIM = 64


def attention_kernel(k_ref, qt_ref, vt_ref, o_ref):
    heads = [slice(h * HEAD_DIM, (h + 1) * HEAD_DIM) for h in range(qt_ref.shape[0] // HEAD_DIM)]
    scores = [jnp.dot(k_ref[:, c], qt_ref[c, :], preferred_element_type=jnp.float32) for c in heads]
    highest = [jnp.max(s, axis=0, keepdims=True) for s in scores]
    exponent = [jnp.exp(s - m) for s, m in zip(scores, highest)]
    denominator = [jnp.sum(e, axis=0, keepdims=True) for e in exponent]
    mixed = [
        jnp.dot(vt_ref[c, :], e.astype(jnp.bfloat16), preferred_element_type=jnp.float32)
        for e, c in zip(exponent, heads)
    ]
    o_ref[...] = jnp.concatenate([m / d for m, d in zip(mixed, denominator)], axis=0).astype(o_ref.dtype)


def attend(keys, queries_t, values_t):
    channels, total = queries_t.shape
    count = keys.shape[0]
    width = channels if total * count * channels <= 256 * 1024 * 640 else 2 * HEAD_DIM
    return pl.pallas_call(
        attention_kernel,
        grid=(channels // width,),
        in_specs=[
            pl.BlockSpec((count, width), lambda j: (0, j)),
            pl.BlockSpec((width, total), lambda j: (j, 0)),
            pl.BlockSpec((width, count), lambda j: (j, 0)),
        ],
        out_specs=pl.BlockSpec((width, total), lambda j: (j, 0)),
        out_shape=jax.ShapeDtypeStruct((channels, total), jnp.bfloat16),
    )(keys, queries_t, values_t)


def extended(array, axis, width):
    size, length = (lax.axis_size(axis), array.shape[0])
    up = [(i, i + 1) for i in range(size - 1)]
    down = [(j, i) for i, j in up]
    last = lax.slice_in_dim(array, length - width, length, axis=0)
    first = lax.slice_in_dim(array, 0, width, axis=0)
    before = lax.ppermute(last, axis, up)
    after = lax.ppermute(first, axis, down)
    return jnp.concatenate([before, array, after], axis=0)


def temporal_mix(padded, weights, count):
    result = jnp.zeros((count * padded.shape[1], padded.shape[2]), jnp.float32)
    for offset in range(3):
        window = padded[offset : offset + count].reshape(-1, padded.shape[2])
        result = result + jnp.dot(window, weights[offset], preferred_element_type=jnp.float32)
    return result


def gather_keyframes(frames, key_index, early):
    n_loc, rows, channels = frames.shape
    fsize = lax.axis_size("frame")
    rsize = lax.axis_size("row")
    me = lax.axis_index("frame")
    last = n_loc * fsize - 1
    other = key_index[0] + key_index[1] - last
    owner_a = other // n_loc
    slot_a = other % n_loc
    owner_b = fsize - 1
    half = rows // 2

    def halves(h):
        return lax.dynamic_slice_in_dim(frames, h * half, half, 1)

    own = halves(me % 2)
    got_a = jnp.where(
        me == owner_a, lax.dynamic_index_in_dim(own, slot_a, 0, keepdims=False), jnp.zeros_like(own[0])
    )
    got_b = own[n_loc - 1]
    for s in sorted(range(1, fsize), key=lambda s: (s != fsize // 2, s)):
        recv = lax.ppermute(halves((me + s) % 2), "frame", [(i, (i + s) % fsize) for i in range(fsize)])
        source = (me - s) % fsize
        got_a = jnp.where(source == owner_a, lax.dynamic_index_in_dim(recv, slot_a, 0, keepdims=False), got_a)
        got_b = jnp.where(source == owner_b, recv[n_loc - 1], got_b)
    piece = jnp.stack([got_a, got_b])
    piece, early = lax.optimization_barrier((piece, early))
    pieces = [piece]
    for s in range(1, rsize):
        pieces.append(lax.ppermute(piece, "row", [(i, (i + s) % rsize) for i in range(rsize)]))
    mine = jnp.stack(pieces).reshape(-1, channels)
    sibling = lax.ppermute(mine, "frame", [(i, i ^ 1) for i in range(fsize)])
    return mine, sibling


def shards(frames, key_index, w_query, w_keyval, w_out, norm_gain, w_first, w_second):
    frame_count, row_count, channels = frames.shape
    assert frame_count >= 2
    flattened = frames.reshape(-1, channels)
    queries_t = lax.dot_general(w_query, flattened, (((0,), (1,)), ((), ())), preferred_element_type=jnp.float32)
    queries_t = (queries_t * HEAD_DIM ** (-0.5)).astype(jnp.bfloat16)
    mine, sibling = gather_keyframes(frames, key_index, queries_t)

    def project(tokens):
        keys = jnp.dot(tokens, w_keyval[:, :channels], preferred_element_type=jnp.float32).astype(jnp.bfloat16)
        values_t = lax.dot_general(
            w_keyval[:, channels:], tokens, (((0,), (1,)), ((), ())), preferred_element_type=jnp.float32
        ).astype(jnp.bfloat16)
        return keys, values_t

    keys_mine, values_mine = project(mine)
    keys_sib, values_sib = project(sibling)
    keys = jnp.concatenate([keys_mine, keys_sib], axis=0)
    values_t = jnp.concatenate([values_mine, values_sib], axis=1)
    attended_t = attend(keys, queries_t, values_t)
    residual = flattened.astype(jnp.float32) + lax.dot_general(
        attended_t, w_out, (((0,), (0,)), ((), ())), preferred_element_type=jnp.float32
    )
    mean_square = jnp.mean(residual * residual, axis=-1, keepdims=True)
    normed = (residual * lax.rsqrt(mean_square + 1e-06) * norm_gain).astype(jnp.bfloat16)
    normed = normed.reshape(frame_count, row_count, channels)
    padded = extended(normed, "frame", 2)
    hidden = jax.nn.silu(temporal_mix(padded, w_first, frame_count + 2)).astype(jnp.bfloat16)
    hidden = hidden.reshape(frame_count + 2, row_count, channels)
    me = lax.axis_index("frame")
    outside = jnp.zeros((1, row_count, channels), hidden.dtype)
    hidden = jnp.concatenate(
        [
            jnp.where(me == 0, outside, hidden[:1]),
            hidden[1:-1],
            jnp.where(me == lax.axis_size("frame") - 1, outside, hidden[-1:]),
        ],
        axis=0,
    )
    second = temporal_mix(hidden, w_second, frame_count)
    return (residual + second).astype(jnp.bfloat16).reshape(frame_count, row_count, channels)


def solution(mesh):
    return jax.shard_map(
        shards,
        mesh=mesh,
        in_specs=(P(("clips", "frame"), "row", None), P("clips"), P(), P(), P(), P(), P(), P()),
        out_specs=P(("clips", "frame"), "row", None),
        check_vma=False,
    )
```

```python
import jax
import jax.numpy as jnp
from jax import lax
from jax.experimental import pallas as pl
from jax.sharding import PartitionSpec as P

HEADS = 10
HEAD_DIM = 64


def attention_kernel(k_ref, qt_ref, vt_ref, o_ref):
    heads = [slice(h * HEAD_DIM, (h + 1) * HEAD_DIM) for h in range(qt_ref.shape[0] // HEAD_DIM)]
    scores = [jnp.dot(k_ref[:, c], qt_ref[c, :], preferred_element_type=jnp.float32) for c in heads]
    highest = [jnp.max(s, axis=0, keepdims=True) for s in scores]
    exponent = [jnp.exp(s - m) for s, m in zip(scores, highest)]
    denominator = [jnp.sum(e, axis=0, keepdims=True) for e in exponent]
    mixed = [
        jnp.dot(vt_ref[c, :], e.astype(jnp.bfloat16), preferred_element_type=jnp.float32)
        for e, c in zip(exponent, heads)
    ]
    o_ref[...] = jnp.concatenate([m / d for m, d in zip(mixed, denominator)], axis=0).astype(o_ref.dtype)


def attend(keys, queries_t, values_t):
    channels, total = queries_t.shape
    count = keys.shape[0]
    width = channels if total * count * channels <= 256 * 1024 * 640 else 2 * HEAD_DIM
    return pl.pallas_call(
        attention_kernel,
        grid=(channels // width,),
        in_specs=[
            pl.BlockSpec((count, width), lambda j: (0, j)),
            pl.BlockSpec((width, total), lambda j: (j, 0)),
            pl.BlockSpec((width, count), lambda j: (j, 0)),
        ],
        out_specs=pl.BlockSpec((width, total), lambda j: (j, 0)),
        out_shape=jax.ShapeDtypeStruct((channels, total), jnp.bfloat16),
    )(keys, queries_t, values_t)


def extended(array, axis, width):
    size, length = (lax.axis_size(axis), array.shape[0])
    up = [(i, i + 1) for i in range(size - 1)]
    down = [(j, i) for i, j in up]
    last = lax.slice_in_dim(array, length - width, length, axis=0)
    first = lax.slice_in_dim(array, 0, width, axis=0)
    before = lax.ppermute(last, axis, up)
    after = lax.ppermute(first, axis, down)
    return jnp.concatenate([before, array, after], axis=0)


def temporal_mix(padded, weights, count):
    result = jnp.zeros((count * padded.shape[1], padded.shape[2]), jnp.float32)
    for offset in range(3):
        window = padded[offset : offset + count].reshape(-1, padded.shape[2])
        result = result + jnp.dot(window, weights[offset], preferred_element_type=jnp.float32)
    return result


def gather_keyframes(frames, key_index, early):
    n_loc, rows, channels = frames.shape
    fsize = lax.axis_size("frame")
    rsize = lax.axis_size("row")
    me = lax.axis_index("frame")
    last = n_loc * fsize - 1
    other = key_index[0] + key_index[1] - last
    owner_a = other // n_loc
    slot_a = other % n_loc
    owner_b = fsize - 1
    half = rows // 2

    def halves(h):
        return lax.dynamic_slice_in_dim(frames, h * half, half, 1)

    own = halves(me % 2)
    got_a = jnp.where(
        me == owner_a, lax.dynamic_index_in_dim(own, slot_a, 0, keepdims=False), jnp.zeros_like(own[0])
    )
    got_b = own[n_loc - 1]
    for s in sorted(range(1, fsize), key=lambda s: (s == fsize // 2, s)):
        recv = lax.ppermute(halves((me + s) % 2), "frame", [(i, (i + s) % fsize) for i in range(fsize)])
        source = (me - s) % fsize
        got_a = jnp.where(source == owner_a, lax.dynamic_index_in_dim(recv, slot_a, 0, keepdims=False), got_a)
        got_b = jnp.where(source == owner_b, recv[n_loc - 1], got_b)
    piece = jnp.stack([got_a, got_b])
    piece, early = lax.optimization_barrier((piece, early))
    pieces = [piece]
    for s in range(1, rsize):
        pieces.append(lax.ppermute(piece, "row", [(i, (i + s) % rsize) for i in range(rsize)]))
    mine = jnp.stack(pieces).reshape(-1, channels)
    sibling = lax.ppermute(mine, "frame", [(i, i ^ 1) for i in range(fsize)])
    return mine, sibling


def shards(frames, key_index, w_query, w_keyval, w_out, norm_gain, w_first, w_second):
    frame_count, row_count, channels = frames.shape
    assert frame_count >= 2
    flattened = frames.reshape(-1, channels)
    queries_t = lax.dot_general(w_query, flattened, (((0,), (1,)), ((), ())), preferred_element_type=jnp.float32)
    queries_t = (queries_t * HEAD_DIM ** (-0.5)).astype(jnp.bfloat16)
    mine, sibling = gather_keyframes(frames, key_index, queries_t)

    def project(tokens):
        keys = jnp.dot(tokens, w_keyval[:, :channels], preferred_element_type=jnp.float32).astype(jnp.bfloat16)
        values_t = lax.dot_general(
            w_keyval[:, channels:], tokens, (((0,), (1,)), ((), ())), preferred_element_type=jnp.float32
        ).astype(jnp.bfloat16)
        return keys, values_t

    keys_mine, values_mine = project(mine)
    keys_sib, values_sib = project(sibling)
    keys = jnp.concatenate([keys_mine, keys_sib], axis=0)
    values_t = jnp.concatenate([values_mine, values_sib], axis=1)
    attended_t = attend(keys, queries_t, values_t)
    residual = flattened.astype(jnp.float32) + lax.dot_general(
        attended_t, w_out, (((0,), (0,)), ((), ())), preferred_element_type=jnp.float32
    )
    mean_square = jnp.mean(residual * residual, axis=-1, keepdims=True)
    normed = (residual * lax.rsqrt(mean_square + 1e-06) * norm_gain).astype(jnp.bfloat16)
    normed = normed.reshape(frame_count, row_count, channels)
    padded = extended(normed, "frame", 2)
    hidden = jax.nn.silu(temporal_mix(padded, w_first, frame_count + 2)).astype(jnp.bfloat16)
    hidden = hidden.reshape(frame_count + 2, row_count, channels)
    me = lax.axis_index("frame")
    outside = jnp.zeros((1, row_count, channels), hidden.dtype)
    hidden = jnp.concatenate(
        [
            jnp.where(me == 0, outside, hidden[:1]),
            hidden[1:-1],
            jnp.where(me == lax.axis_size("frame") - 1, outside, hidden[-1:]),
        ],
        axis=0,
    )
    second = temporal_mix(hidden, w_second, frame_count)
    return (residual + second).astype(jnp.bfloat16).reshape(frame_count, row_count, channels)


def solution(mesh):
    return jax.shard_map(
        shards,
        mesh=mesh,
        in_specs=(P(("clips", "frame"), "row", None), P("clips"), P(), P(), P(), P(), P(), P()),
        out_specs=P(("clips", "frame"), "row", None),
        check_vma=False,
    )
```

```python
import jax
import jax.numpy as jnp
from jax import lax
from jax.experimental import pallas as pl
from jax.sharding import PartitionSpec as P

HEADS = 10
HEAD_DIM = 64


def attention_kernel(k_ref, qt_ref, vt_ref, o_ref):
    heads = [slice(h * HEAD_DIM, (h + 1) * HEAD_DIM) for h in range(qt_ref.shape[0] // HEAD_DIM)]
    scores = [jnp.dot(k_ref[:, c], qt_ref[c, :], preferred_element_type=jnp.float32) for c in heads]
    highest = [jnp.max(s, axis=0, keepdims=True) for s in scores]
    exponent = [jnp.exp(s - m) for s, m in zip(scores, highest)]
    denominator = [jnp.sum(e, axis=0, keepdims=True) for e in exponent]
    mixed = [
        jnp.dot(vt_ref[c, :], e.astype(jnp.bfloat16), preferred_element_type=jnp.float32)
        for e, c in zip(exponent, heads)
    ]
    o_ref[...] = jnp.concatenate([m / d for m, d in zip(mixed, denominator)], axis=0).astype(o_ref.dtype)


def attend(keys, queries_t, values_t):
    channels, total = queries_t.shape
    count = keys.shape[0]
    width = channels if total * count * channels <= 256 * 1024 * 640 else 2 * HEAD_DIM
    return pl.pallas_call(
        attention_kernel,
        grid=(channels // width,),
        in_specs=[
            pl.BlockSpec((count, width), lambda j: (0, j)),
            pl.BlockSpec((width, total), lambda j: (j, 0)),
            pl.BlockSpec((width, count), lambda j: (j, 0)),
        ],
        out_specs=pl.BlockSpec((width, total), lambda j: (j, 0)),
        out_shape=jax.ShapeDtypeStruct((channels, total), jnp.bfloat16),
    )(keys, queries_t, values_t)


def extended(array, axis, width):
    size, length = (lax.axis_size(axis), array.shape[0])
    up = [(i, i + 1) for i in range(size - 1)]
    down = [(j, i) for i, j in up]
    last = lax.slice_in_dim(array, length - width, length, axis=0)
    first = lax.slice_in_dim(array, 0, width, axis=0)
    before = lax.ppermute(last, axis, up)
    after = lax.ppermute(first, axis, down)
    return jnp.concatenate([before, array, after], axis=0)


def temporal_mix(padded, weights, count):
    result = jnp.zeros((count * padded.shape[1], padded.shape[2]), jnp.float32)
    for offset in range(3):
        window = padded[offset : offset + count].reshape(-1, padded.shape[2])
        result = result + jnp.dot(window, weights[offset], preferred_element_type=jnp.float32)
    return result


def gather_keyframes(frames, key_index, early):
    n_loc, rows, channels = frames.shape
    fsize = lax.axis_size("frame")
    rsize = lax.axis_size("row")
    me = lax.axis_index("frame")
    last = n_loc * fsize - 1
    other = key_index[0] + key_index[1] - last
    owner_a = other // n_loc
    slot_a = other % n_loc
    owner_b = fsize - 1
    half = rows // 2

    def halves(h):
        return lax.dynamic_slice_in_dim(frames, h * half, half, 1)

    own = halves(me % 2)
    got_a = jnp.where(
        me == owner_a, lax.dynamic_index_in_dim(own, slot_a, 0, keepdims=False), jnp.zeros_like(own[0])
    )
    got_b = own[n_loc - 1]
    for s in reversed(range(1, fsize)):
        recv = lax.ppermute(halves((me + s) % 2), "frame", [(i, (i + s) % fsize) for i in range(fsize)])
        source = (me - s) % fsize
        got_a = jnp.where(source == owner_a, lax.dynamic_index_in_dim(recv, slot_a, 0, keepdims=False), got_a)
        got_b = jnp.where(source == owner_b, recv[n_loc - 1], got_b)
    piece = jnp.stack([got_a, got_b])
    piece, early = lax.optimization_barrier((piece, early))
    pieces = [piece]
    for s in range(1, rsize):
        pieces.append(lax.ppermute(piece, "row", [(i, (i + s) % rsize) for i in range(rsize)]))
    mine = jnp.stack(pieces).reshape(-1, channels)
    sibling = lax.ppermute(mine, "frame", [(i, i ^ 1) for i in range(fsize)])
    return mine, sibling


def shards(frames, key_index, w_query, w_keyval, w_out, norm_gain, w_first, w_second):
    frame_count, row_count, channels = frames.shape
    assert frame_count >= 2
    flattened = frames.reshape(-1, channels)
    queries_t = lax.dot_general(w_query, flattened, (((0,), (1,)), ((), ())), preferred_element_type=jnp.float32)
    queries_t = (queries_t * HEAD_DIM ** (-0.5)).astype(jnp.bfloat16)
    mine, sibling = gather_keyframes(frames, key_index, queries_t)

    def project(tokens):
        keys = jnp.dot(tokens, w_keyval[:, :channels], preferred_element_type=jnp.float32).astype(jnp.bfloat16)
        values_t = lax.dot_general(
            w_keyval[:, channels:], tokens, (((0,), (1,)), ((), ())), preferred_element_type=jnp.float32
        ).astype(jnp.bfloat16)
        return keys, values_t

    keys_mine, values_mine = project(mine)
    keys_sib, values_sib = project(sibling)
    keys = jnp.concatenate([keys_mine, keys_sib], axis=0)
    values_t = jnp.concatenate([values_mine, values_sib], axis=1)
    attended_t = attend(keys, queries_t, values_t)
    residual = flattened.astype(jnp.float32) + lax.dot_general(
        attended_t, w_out, (((0,), (0,)), ((), ())), preferred_element_type=jnp.float32
    )
    mean_square = jnp.mean(residual * residual, axis=-1, keepdims=True)
    normed = (residual * lax.rsqrt(mean_square + 1e-06) * norm_gain).astype(jnp.bfloat16)
    normed = normed.reshape(frame_count, row_count, channels)
    padded = extended(normed, "frame", 2)
    hidden = jax.nn.silu(temporal_mix(padded, w_first, frame_count + 2)).astype(jnp.bfloat16)
    hidden = hidden.reshape(frame_count + 2, row_count, channels)
    me = lax.axis_index("frame")
    outside = jnp.zeros((1, row_count, channels), hidden.dtype)
    hidden = jnp.concatenate(
        [
            jnp.where(me == 0, outside, hidden[:1]),
            hidden[1:-1],
            jnp.where(me == lax.axis_size("frame") - 1, outside, hidden[-1:]),
        ],
        axis=0,
    )
    second = temporal_mix(hidden, w_second, frame_count)
    return (residual + second).astype(jnp.bfloat16).reshape(frame_count, row_count, channels)


def solution(mesh):
    return jax.shard_map(
        shards,
        mesh=mesh,
        in_specs=(P(("clips", "frame"), "row", None), P("clips"), P(), P(), P(), P(), P(), P()),
        out_specs=P(("clips", "frame"), "row", None),
        check_vma=False,
    )
```

```python
import jax
import jax.numpy as jnp
from jax import lax
from jax.experimental import pallas as pl
from jax.sharding import PartitionSpec as P

HEADS = 10
HEAD_DIM = 64


def attention_kernel(k_ref, qt_ref, vt_ref, o_ref):
    heads = [slice(h * HEAD_DIM, (h + 1) * HEAD_DIM) for h in range(qt_ref.shape[0] // HEAD_DIM)]
    scores = [jnp.dot(k_ref[:, c], qt_ref[c, :], preferred_element_type=jnp.float32) for c in heads]
    highest = [jnp.max(s, axis=0, keepdims=True) for s in scores]
    exponent = [jnp.exp(s - m) for s, m in zip(scores, highest)]
    denominator = [jnp.sum(e, axis=0, keepdims=True) for e in exponent]
    mixed = [
        jnp.dot(vt_ref[c, :], e.astype(jnp.bfloat16), preferred_element_type=jnp.float32)
        for e, c in zip(exponent, heads)
    ]
    o_ref[...] = jnp.concatenate([m / d for m, d in zip(mixed, denominator)], axis=0).astype(o_ref.dtype)


def attend(keys, queries_t, values_t):
    channels, total = queries_t.shape
    count = keys.shape[0]
    width = channels if total * count * channels <= 256 * 1024 * 640 else 2 * HEAD_DIM
    return pl.pallas_call(
        attention_kernel,
        grid=(channels // width,),
        in_specs=[
            pl.BlockSpec((count, width), lambda j: (0, j)),
            pl.BlockSpec((width, total), lambda j: (j, 0)),
            pl.BlockSpec((width, count), lambda j: (j, 0)),
        ],
        out_specs=pl.BlockSpec((width, total), lambda j: (j, 0)),
        out_shape=jax.ShapeDtypeStruct((channels, total), jnp.bfloat16),
    )(keys, queries_t, values_t)


def extended(array, axis, width):
    size, length = (lax.axis_size(axis), array.shape[0])
    up = [(i, i + 1) for i in range(size - 1)]
    down = [(j, i) for i, j in up]
    last = lax.slice_in_dim(array, length - width, length, axis=0)
    first = lax.slice_in_dim(array, 0, width, axis=0)
    before = lax.ppermute(last, axis, up)
    after = lax.ppermute(first, axis, down)
    return jnp.concatenate([before, array, after], axis=0)


def temporal_mix(padded, weights, count):
    result = jnp.zeros((count * padded.shape[1], padded.shape[2]), jnp.float32)
    for offset in range(3):
        window = padded[offset : offset + count].reshape(-1, padded.shape[2])
        result = result + jnp.dot(window, weights[offset], preferred_element_type=jnp.float32)
    return result


def gather_keyframes(frames, key_index, early):
    n_loc, rows, channels = frames.shape
    fsize = lax.axis_size("frame")
    rsize = lax.axis_size("row")
    me = lax.axis_index("frame")
    last = n_loc * fsize - 1
    other = key_index[0] + key_index[1] - last
    owner_a = other // n_loc
    slot_a = other % n_loc
    owner_b = fsize - 1
    half = rows // 2

    def halves(h):
        return lax.dynamic_slice_in_dim(frames, h * half, half, 1)

    own = halves(me % 2)
    got_a = jnp.where(
        me == owner_a, lax.dynamic_index_in_dim(own, slot_a, 0, keepdims=False), jnp.zeros_like(own[0])
    )
    got_b = own[n_loc - 1]
    for s in sorted(range(1, fsize), key=lambda s: (s == fsize // 2, -s)):
        recv = lax.ppermute(halves((me + s) % 2), "frame", [(i, (i + s) % fsize) for i in range(fsize)])
        source = (me - s) % fsize
        got_a = jnp.where(source == owner_a, lax.dynamic_index_in_dim(recv, slot_a, 0, keepdims=False), got_a)
        got_b = jnp.where(source == owner_b, recv[n_loc - 1], got_b)
    piece = jnp.stack([got_a, got_b])
    piece, early = lax.optimization_barrier((piece, early))
    pieces = [piece]
    for s in range(1, rsize):
        pieces.append(lax.ppermute(piece, "row", [(i, (i + s) % rsize) for i in range(rsize)]))
    mine = jnp.stack(pieces).reshape(-1, channels)
    sibling = lax.ppermute(mine, "frame", [(i, i ^ 1) for i in range(fsize)])
    return mine, sibling


def shards(frames, key_index, w_query, w_keyval, w_out, norm_gain, w_first, w_second):
    frame_count, row_count, channels = frames.shape
    assert frame_count >= 2
    flattened = frames.reshape(-1, channels)
    queries_t = lax.dot_general(w_query, flattened, (((0,), (1,)), ((), ())), preferred_element_type=jnp.float32)
    queries_t = (queries_t * HEAD_DIM ** (-0.5)).astype(jnp.bfloat16)
    mine, sibling = gather_keyframes(frames, key_index, queries_t)

    def project(tokens):
        keys = jnp.dot(tokens, w_keyval[:, :channels], preferred_element_type=jnp.float32).astype(jnp.bfloat16)
        values_t = lax.dot_general(
            w_keyval[:, channels:], tokens, (((0,), (1,)), ((), ())), preferred_element_type=jnp.float32
        ).astype(jnp.bfloat16)
        return keys, values_t

    keys_mine, values_mine = project(mine)
    keys_sib, values_sib = project(sibling)
    keys = jnp.concatenate([keys_mine, keys_sib], axis=0)
    values_t = jnp.concatenate([values_mine, values_sib], axis=1)
    attended_t = attend(keys, queries_t, values_t)
    residual = flattened.astype(jnp.float32) + lax.dot_general(
        attended_t, w_out, (((0,), (0,)), ((), ())), preferred_element_type=jnp.float32
    )
    mean_square = jnp.mean(residual * residual, axis=-1, keepdims=True)
    normed = (residual * lax.rsqrt(mean_square + 1e-06) * norm_gain).astype(jnp.bfloat16)
    normed = normed.reshape(frame_count, row_count, channels)
    padded = extended(normed, "frame", 2)
    hidden = jax.nn.silu(temporal_mix(padded, w_first, frame_count + 2)).astype(jnp.bfloat16)
    hidden = hidden.reshape(frame_count + 2, row_count, channels)
    me = lax.axis_index("frame")
    outside = jnp.zeros((1, row_count, channels), hidden.dtype)
    hidden = jnp.concatenate(
        [
            jnp.where(me == 0, outside, hidden[:1]),
            hidden[1:-1],
            jnp.where(me == lax.axis_size("frame") - 1, outside, hidden[-1:]),
        ],
        axis=0,
    )
    second = temporal_mix(hidden, w_second, frame_count)
    return (residual + second).astype(jnp.bfloat16).reshape(frame_count, row_count, channels)


def solution(mesh):
    return jax.shard_map(
        shards,
        mesh=mesh,
        in_specs=(P(("clips", "frame"), "row", None), P("clips"), P(), P(), P(), P(), P(), P()),
        out_specs=P(("clips", "frame"), "row", None),
        check_vma=False,
    )
```

```python
import jax
import jax.numpy as jnp
from jax import lax
from jax.experimental import pallas as pl
from jax.sharding import PartitionSpec as P

HEADS = 10
HEAD_DIM = 64


def attention_kernel(k_ref, qt_ref, vt_ref, o_ref):
    heads = [slice(h * HEAD_DIM, (h + 1) * HEAD_DIM) for h in range(qt_ref.shape[0] // HEAD_DIM)]
    scores = [jnp.dot(k_ref[:, c], qt_ref[c, :], preferred_element_type=jnp.float32) for c in heads]
    highest = [jnp.max(s, axis=0, keepdims=True) for s in scores]
    exponent = [jnp.exp(s - m) for s, m in zip(scores, highest)]
    denominator = [jnp.sum(e, axis=0, keepdims=True) for e in exponent]
    mixed = [
        jnp.dot(vt_ref[c, :], e.astype(jnp.bfloat16), preferred_element_type=jnp.float32)
        for e, c in zip(exponent, heads)
    ]
    o_ref[...] = jnp.concatenate([m / d for m, d in zip(mixed, denominator)], axis=0).astype(o_ref.dtype)


def attend(keys, queries_t, values_t):
    channels, total = queries_t.shape
    count = keys.shape[0]
    width = channels if total * count * channels <= 256 * 1024 * 640 else 2 * HEAD_DIM
    return pl.pallas_call(
        attention_kernel,
        grid=(channels // width,),
        in_specs=[
            pl.BlockSpec((count, width), lambda j: (0, j)),
            pl.BlockSpec((width, total), lambda j: (j, 0)),
            pl.BlockSpec((width, count), lambda j: (j, 0)),
        ],
        out_specs=pl.BlockSpec((width, total), lambda j: (j, 0)),
        out_shape=jax.ShapeDtypeStruct((channels, total), jnp.bfloat16),
    )(keys, queries_t, values_t)


def extended(array, axis, width):
    size, length = (lax.axis_size(axis), array.shape[0])
    up = [(i, i + 1) for i in range(size - 1)]
    down = [(j, i) for i, j in up]
    last = lax.slice_in_dim(array, length - width, length, axis=0)
    first = lax.slice_in_dim(array, 0, width, axis=0)
    before = lax.ppermute(last, axis, up)
    after = lax.ppermute(first, axis, down)
    return jnp.concatenate([before, array, after], axis=0)


def temporal_mix(padded, weights, count):
    result = jnp.zeros((count * padded.shape[1], padded.shape[2]), jnp.float32)
    for offset in range(3):
        window = padded[offset : offset + count].reshape(-1, padded.shape[2])
        result = result + jnp.dot(window, weights[offset], preferred_element_type=jnp.float32)
    return result


def gather_keyframes(frames, key_index, early):
    n_loc, rows, channels = frames.shape
    fsize = lax.axis_size("frame")
    rsize = lax.axis_size("row")
    me = lax.axis_index("frame")
    last = n_loc * fsize - 1
    other = key_index[0] + key_index[1] - last
    owner_a = other // n_loc
    slot_a = other % n_loc
    owner_b = fsize - 1
    half = rows // 2

    def halves(h):
        return lax.dynamic_slice_in_dim(frames, h * half, half, 1)

    own = halves(me % 2)
    got_a = jnp.where(
        me == owner_a, lax.dynamic_index_in_dim(own, slot_a, 0, keepdims=False), jnp.zeros_like(own[0])
    )
    got_b = own[n_loc - 1]
    for s in sorted(range(1, fsize), key=lambda s: (s != fsize // 2, -s)):
        recv = lax.ppermute(halves((me + s) % 2), "frame", [(i, (i + s) % fsize) for i in range(fsize)])
        source = (me - s) % fsize
        got_a = jnp.where(source == owner_a, lax.dynamic_index_in_dim(recv, slot_a, 0, keepdims=False), got_a)
        got_b = jnp.where(source == owner_b, recv[n_loc - 1], got_b)
    piece = jnp.stack([got_a, got_b])
    piece, early = lax.optimization_barrier((piece, early))
    pieces = [piece]
    for s in range(1, rsize):
        pieces.append(lax.ppermute(piece, "row", [(i, (i + s) % rsize) for i in range(rsize)]))
    mine = jnp.stack(pieces).reshape(-1, channels)
    sibling = lax.ppermute(mine, "frame", [(i, i ^ 1) for i in range(fsize)])
    return mine, sibling


def shards(frames, key_index, w_query, w_keyval, w_out, norm_gain, w_first, w_second):
    frame_count, row_count, channels = frames.shape
    assert frame_count >= 2
    flattened = frames.reshape(-1, channels)
    queries_t = lax.dot_general(w_query, flattened, (((0,), (1,)), ((), ())), preferred_element_type=jnp.float32)
    queries_t = (queries_t * HEAD_DIM ** (-0.5)).astype(jnp.bfloat16)
    mine, sibling = gather_keyframes(frames, key_index, queries_t)

    def project(tokens):
        keys = jnp.dot(tokens, w_keyval[:, :channels], preferred_element_type=jnp.float32).astype(jnp.bfloat16)
        values_t = lax.dot_general(
            w_keyval[:, channels:], tokens, (((0,), (1,)), ((), ())), preferred_element_type=jnp.float32
        ).astype(jnp.bfloat16)
        return keys, values_t

    keys_mine, values_mine = project(mine)
    keys_sib, values_sib = project(sibling)
    keys = jnp.concatenate([keys_mine, keys_sib], axis=0)
    values_t = jnp.concatenate([values_mine, values_sib], axis=1)
    attended_t = attend(keys, queries_t, values_t)
    residual = flattened.astype(jnp.float32) + lax.dot_general(
        attended_t, w_out, (((0,), (0,)), ((), ())), preferred_element_type=jnp.float32
    )
    mean_square = jnp.mean(residual * residual, axis=-1, keepdims=True)
    normed = (residual * lax.rsqrt(mean_square + 1e-06) * norm_gain).astype(jnp.bfloat16)
    normed = normed.reshape(frame_count, row_count, channels)
    padded = extended(normed, "frame", 2)
    hidden = jax.nn.silu(temporal_mix(padded, w_first, frame_count + 2)).astype(jnp.bfloat16)
    hidden = hidden.reshape(frame_count + 2, row_count, channels)
    me = lax.axis_index("frame")
    outside = jnp.zeros((1, row_count, channels), hidden.dtype)
    hidden = jnp.concatenate(
        [
            jnp.where(me == 0, outside, hidden[:1]),
            hidden[1:-1],
            jnp.where(me == lax.axis_size("frame") - 1, outside, hidden[-1:]),
        ],
        axis=0,
    )
    second = temporal_mix(hidden, w_second, frame_count)
    return (residual + second).astype(jnp.bfloat16).reshape(frame_count, row_count, channels)


def solution(mesh):
    return jax.shard_map(
        shards,
        mesh=mesh,
        in_specs=(P(("clips", "frame"), "row", None), P("clips"), P(), P(), P(), P(), P(), P()),
        out_specs=P(("clips", "frame"), "row", None),
        check_vma=False,
    )
```

```python
import jax
import jax.numpy as jnp
from jax import lax
from jax.experimental import pallas as pl
from jax.sharding import PartitionSpec as P

HEADS = 10
HEAD_DIM = 64


def attention_kernel(k_ref, qt_ref, vt_ref, o_ref):
    heads = [slice(h * HEAD_DIM, (h + 1) * HEAD_DIM) for h in range(qt_ref.shape[0] // HEAD_DIM)]
    scores = [jnp.dot(k_ref[:, c], qt_ref[c, :], preferred_element_type=jnp.float32) for c in heads]
    highest = [jnp.max(s, axis=0, keepdims=True) for s in scores]
    exponent = [jnp.exp(s - m) for s, m in zip(scores, highest)]
    denominator = [jnp.sum(e, axis=0, keepdims=True) for e in exponent]
    mixed = [
        jnp.dot(vt_ref[c, :], e.astype(jnp.bfloat16), preferred_element_type=jnp.float32)
        for e, c in zip(exponent, heads)
    ]
    o_ref[...] = jnp.concatenate([m / d for m, d in zip(mixed, denominator)], axis=0).astype(o_ref.dtype)


def attend(keys, queries_t, values_t):
    channels, total = queries_t.shape
    count = keys.shape[0]
    width = channels if total * count * channels <= 256 * 1024 * 640 else 2 * HEAD_DIM
    return pl.pallas_call(
        attention_kernel,
        grid=(channels // width,),
        in_specs=[
            pl.BlockSpec((count, width), lambda j: (0, j)),
            pl.BlockSpec((width, total), lambda j: (j, 0)),
            pl.BlockSpec((width, count), lambda j: (j, 0)),
        ],
        out_specs=pl.BlockSpec((width, total), lambda j: (j, 0)),
        out_shape=jax.ShapeDtypeStruct((channels, total), jnp.bfloat16),
    )(keys, queries_t, values_t)


def extended(array, axis, width):
    size, length = (lax.axis_size(axis), array.shape[0])
    up = [(i, i + 1) for i in range(size - 1)]
    down = [(j, i) for i, j in up]
    last = lax.slice_in_dim(array, length - width, length, axis=0)
    first = lax.slice_in_dim(array, 0, width, axis=0)
    before = lax.ppermute(last, axis, up)
    after = lax.ppermute(first, axis, down)
    return jnp.concatenate([before, array, after], axis=0)


def temporal_mix(padded, weights, count):
    result = jnp.zeros((count * padded.shape[1], padded.shape[2]), jnp.float32)
    for offset in range(3):
        window = padded[offset : offset + count].reshape(-1, padded.shape[2])
        result = result + jnp.dot(window, weights[offset], preferred_element_type=jnp.float32)
    return result


def gather_keyframes(frames, key_index, early):
    n_loc, rows, channels = frames.shape
    fsize = lax.axis_size("frame")
    rsize = lax.axis_size("row")
    me = lax.axis_index("frame")
    last = n_loc * fsize - 1
    other = key_index[0] + key_index[1] - last
    owner_a = other // n_loc
    slot_a = other % n_loc
    owner_b = fsize - 1
    half = rows // 2

    def halves(h):
        return lax.dynamic_slice_in_dim(frames, h * half, half, 1)

    own = halves(me % 2)
    got_a = jnp.where(
        me == owner_a, lax.dynamic_index_in_dim(own, slot_a, 0, keepdims=False), jnp.zeros_like(own[0])
    )
    got_b = own[n_loc - 1]
    for s in range(1, fsize):
        recv = lax.ppermute(halves((me + s) % 2), "frame", [(i, (i + s) % fsize) for i in range(fsize)])
        source = (me - s) % fsize
        got_a = jnp.where(source == owner_a, lax.dynamic_index_in_dim(recv, slot_a, 0, keepdims=False), got_a)
        got_b = jnp.where(source == owner_b, recv[n_loc - 1], got_b)
    piece = jnp.stack([got_a, got_b])
    piece, early = lax.optimization_barrier((piece, early))
    pieces = [piece]
    for s in reversed(range(1, rsize)):
        pieces.append(lax.ppermute(piece, "row", [(i, (i + s) % rsize) for i in range(rsize)]))
    mine = jnp.stack(pieces).reshape(-1, channels)
    sibling = lax.ppermute(mine, "frame", [(i, i ^ 1) for i in range(fsize)])
    return mine, sibling


def shards(frames, key_index, w_query, w_keyval, w_out, norm_gain, w_first, w_second):
    frame_count, row_count, channels = frames.shape
    assert frame_count >= 2
    flattened = frames.reshape(-1, channels)
    queries_t = lax.dot_general(w_query, flattened, (((0,), (1,)), ((), ())), preferred_element_type=jnp.float32)
    queries_t = (queries_t * HEAD_DIM ** (-0.5)).astype(jnp.bfloat16)
    mine, sibling = gather_keyframes(frames, key_index, queries_t)

    def project(tokens):
        keys = jnp.dot(tokens, w_keyval[:, :channels], preferred_element_type=jnp.float32).astype(jnp.bfloat16)
        values_t = lax.dot_general(
            w_keyval[:, channels:], tokens, (((0,), (1,)), ((), ())), preferred_element_type=jnp.float32
        ).astype(jnp.bfloat16)
        return keys, values_t

    keys_mine, values_mine = project(mine)
    keys_sib, values_sib = project(sibling)
    keys = jnp.concatenate([keys_mine, keys_sib], axis=0)
    values_t = jnp.concatenate([values_mine, values_sib], axis=1)
    attended_t = attend(keys, queries_t, values_t)
    residual = flattened.astype(jnp.float32) + lax.dot_general(
        attended_t, w_out, (((0,), (0,)), ((), ())), preferred_element_type=jnp.float32
    )
    mean_square = jnp.mean(residual * residual, axis=-1, keepdims=True)
    normed = (residual * lax.rsqrt(mean_square + 1e-06) * norm_gain).astype(jnp.bfloat16)
    normed = normed.reshape(frame_count, row_count, channels)
    padded = extended(normed, "frame", 2)
    hidden = jax.nn.silu(temporal_mix(padded, w_first, frame_count + 2)).astype(jnp.bfloat16)
    hidden = hidden.reshape(frame_count + 2, row_count, channels)
    me = lax.axis_index("frame")
    outside = jnp.zeros((1, row_count, channels), hidden.dtype)
    hidden = jnp.concatenate(
        [
            jnp.where(me == 0, outside, hidden[:1]),
            hidden[1:-1],
            jnp.where(me == lax.axis_size("frame") - 1, outside, hidden[-1:]),
        ],
        axis=0,
    )
    second = temporal_mix(hidden, w_second, frame_count)
    return (residual + second).astype(jnp.bfloat16).reshape(frame_count, row_count, channels)


def solution(mesh):
    return jax.shard_map(
        shards,
        mesh=mesh,
        in_specs=(P(("clips", "frame"), "row", None), P("clips"), P(), P(), P(), P(), P(), P()),
        out_specs=P(("clips", "frame"), "row", None),
        check_vma=False,
    )
```
